32 devices in a mesh: comp: 4 (over y, x), band: 8 (over z, core).
Axes of the slice: x: 2, y: 2, z: 4, core: 2. Of those that a mesh axis runs over, the one named last changes fastest.
Arguments:
- estimate: float32 [512, 256], P('band'), may hold values from -6 to 6
- residual: float32 [512, 256], P('band'), may hold values from -50 to 50
- direction: float32 [512, 256], P('band'), may hold values from -50 to 50
- kernels: bfloat16 [32, 65, 65], P('comp'), may hold values from -0.015625 to 0.015625
- weight_maps: bfloat16 [32, 512, 256], P('comp', 'band'), may hold values from -6 to 6
- filters_in: float32 [64, 3, 3], replicated, may hold values from -2 to 2
- biases: float32 [64], replicated, may hold values from -3 to 3
- filters_out: float32 [64, 3, 3], replicated, may hold values from -0.25 to 0.25
Outputs:
- estimate_next: float32 [512, 256], P('band')
- residual_next: float32 [512, 256], P('band')
- direction_next: float32 [512, 256], P('band')
- denoised: float32 [512, 256], P('band', 'comp')
The draws below stay inside these ranges and needn't reach their ends.
All inputs are finite; a program needn't handle non-finite values.
Results may differ from the reference program's by a relative error of at most 0.0024.
Values may be sent and summed in bfloat16 or wider, within the bound.
No kernel may reach another device: no remote copies, remote signals or barrier semaphores. Data moves between devices by JAX's collectives and lax.ppermute only.
A program may use at most 64 MiB of HBM per device.

```python
import jax
import jax.numpy as jnp
from jax import lax

K = 32
P_SIZE = 65
C = 64
W = 256
HALF = 32
H = 512


def field_scales(key):
    rows = jnp.arange(H, dtype=jnp.float32) / max(H - 1, 1)
    column_exps = jax.random.uniform(jax.random.fold_in(key, 11), (W,), jnp.float32)
    return (10.0 ** rows)[:, None] * (10.0 ** column_exps)[None, :] / 10.0


def field_noise(key, salt):
    noise = jnp.clip(jax.random.normal(jax.random.fold_in(key, salt), (H, W), jnp.float32), -5.0, 5.0)
    return noise * field_scales(key)


def draw_residual(key, part):
    return field_noise(key, 21)


def draw_direction(key, part):
    return field_noise(key, 22)


def level_of(key, shape, cuts, least, largest):
    factor_of, own = 1.0, jax.random.fold_in(key, 6)
    for position, shards_of in cuts:
        steps = jnp.exp(jax.random.uniform(jax.random.fold_in(own, position), (shards_of,), jnp.float32, least / len(cuts), largest / len(cuts)))
        factor_of = factor_of * jnp.repeat(steps, shape[position] // shards_of).reshape([-1 if axis == position else 1 for axis in range(len(shape))])
    return factor_of


def bell_draw(key, shape, spread, limit, split=(), held_as=jnp.bfloat16):
    values = jax.random.normal(key, shape, jnp.float32) * spread
    if len(split) > 0:
        values = level_of(key, shape, split, -0.22, 0.18) * values
    return jnp.clip(values, min=-limit, max=limit).astype(held_as)


def setup_inputs(seed: int = 0) -> dict:
    keys = jax.random.split(jax.random.key(seed), 9)
    return {
        "estimate": bell_draw(keys[0], (H, W), 1.0, 6.0, ((0, 8),), jnp.float32),
        "residual": draw_residual(jax.random.fold_in(keys[8], 71), 0),
        "direction": draw_direction(jax.random.fold_in(keys[8], 71), 0),
        "kernels": bell_draw(keys[3], (K, P_SIZE, P_SIZE), (K * P_SIZE * P_SIZE) ** -0.5, 0.015625, ((0, 4),)),
        "weight_maps": bell_draw(keys[4], (K, H, W), 1.0, 6.0, ((0, 4), (1, 8))),
        "filters_in": bell_draw(keys[5], (C, 3, 3), 9 ** -0.5, 2.0, (), jnp.float32),
        "biases": bell_draw(keys[6], (C,), 0.5, 3.0, (), jnp.float32),
        "filters_out": bell_draw(keys[7], (C, 3, 3), (9 * C) ** -0.5, 0.25, (), jnp.float32),
    }


damping = 0.5
numbers = ("NCHW", "OIHW", "NCHW")


def reference(estimate, residual, direction, kernels, weight_maps, filters_in, biases, filters_out):
    maps_wide = weight_maps.astype(jnp.float32)
    shaped = (maps_wide * direction[None]).astype(jnp.bfloat16)
    image = lax.conv_general_dilated(shaped[None], kernels[None], (1, 1), [(HALF, HALF), (HALF, HALF)], dimension_numbers=numbers, preferred_element_type=jnp.float32)[0, 0]
    image = image.astype(jnp.bfloat16)
    flipped = kernels[:, None, ::-1, ::-1]
    back = lax.conv_general_dilated(image[None, None], flipped, (1, 1), [(HALF, HALF), (HALF, HALF)], dimension_numbers=numbers, preferred_element_type=jnp.float32)[0]
    normal = jnp.sum(maps_wide * back, axis=0)
    curved = normal + damping * direction
    old = jnp.sum(residual * residual)
    alpha = old / jnp.sum(direction * curved)
    estimate_next = estimate + alpha * direction
    residual_next = residual - alpha * curved
    new = jnp.sum(residual_next * residual_next)
    direction_next = residual_next + (new / old) * direction
    features = lax.conv_general_dilated(estimate_next[None, None], filters_in[:, None], (1, 1), [(1, 1), (1, 1)], dimension_numbers=numbers, precision=lax.Precision.HIGHEST)
    features = jax.nn.relu(features + biases[None, :, None, None])
    mixed = lax.conv_general_dilated(features, filters_out[None], (1, 1), [(1, 1), (1, 1)], dimension_numbers=numbers, precision=lax.Precision.HIGHEST)[0, 0]
    denoised = estimate_next - mixed
    return estimate_next, residual_next, direction_next, denoised
```

```python
import functools

import jax
import jax.numpy as jnp
from jax import lax
from jax.experimental import pallas as pl
from jax.experimental.pallas import tpu as pltpu
from jax.sharding import PartitionSpec as P

damping = 0.5
LANES = 128


def with_halo(array, sides, width):
    for axis, dim in sides:
        count, length = (lax.axis_size(axis), array.shape[dim])
        up = [(i, (i + 1) % count) for i in range(count - 1)]
        down = [(j, i) for i, j in up]
        last = lax.slice_in_dim(array, length - width, length, axis=dim)
        first = lax.slice_in_dim(array, 0, width, axis=dim)
        before = lax.ppermute(last, axis, up)
        after = lax.ppermute(first, axis, down)
        array = jnp.concatenate([before, array, after], axis=dim)
    return array


def denoise(estimate_next, filters_in, biases, filters_out):
    rows, width = estimate_next.shape
    framed = with_halo(estimate_next, (("band", 0),), 2)
    columns = width // lax.axis_size("comp")
    start = lax.axis_index("comp") * columns
    padded = jnp.pad(framed, ((0, 0), (2, 2)))
    tile = lax.dynamic_slice_in_dim(padded, start, columns + 4, 1)
    taps = jnp.stack(
        [tile[a : a + rows + 2, b : b + columns + 2] for a in range(3) for b in range(3)]
    )
    channels = filters_in.shape[0]
    features = jnp.einsum(
        "ct,tij->cij", filters_in.reshape(channels, 9), taps, precision=lax.Precision.HIGHEST
    )
    features = jax.nn.relu(features + biases[:, None, None])
    total_rows = rows * lax.axis_size("band")
    global_rows = lax.axis_index("band") * rows - 1 + jnp.arange(rows + 2)
    global_cols = start - 1 + jnp.arange(columns + 2)
    inside_rows = (global_rows >= 0) & (global_rows < total_rows)
    inside_cols = (global_cols >= 0) & (global_cols < width)
    inside = (inside_rows[:, None] & inside_cols[None, :]).astype(jnp.float32)
    features = features * inside[None]
    spread = jnp.einsum(
        "ct,cij->tij", filters_out.reshape(channels, 9), features, precision=lax.Precision.HIGHEST
    )
    mixed = sum(
        (spread[a * 3 + b, a : a + rows, b : b + columns] for a in range(3) for b in range(3))
    )
    return tile[2 : 2 + rows, 2 : 2 + columns] - mixed


def tap_rows(kernels):
    span = kernels.shape[2]
    idx = (LANES - jnp.arange(LANES)) % LANES
    taps = kernels.astype(jnp.float32)[:, :, jnp.clip(idx, 0, span - 1)]
    return jnp.where((idx < span)[None, None], taps, 0.0)


def _toeplitz(g, valid):
    t = pltpu.roll(jnp.broadcast_to(g, valid.shape), 0, 1, stride=1, stride_axis=0)
    return jnp.where(valid, t, 0.0).astype(jnp.bfloat16)


def _band(span):
    p = lax.broadcasted_iota(jnp.int32, (2 * LANES, LANES), 0)
    v = lax.broadcasted_iota(jnp.int32, (2 * LANES, LANES), 1)
    d = p - v
    return (d >= 0) & (d < span)


def _lhs(part, r, rows, blocks):
    pieces = [part[r : r + rows, n * LANES : n * LANES + 2 * LANES] for n in range(blocks)]
    return jnp.concatenate(pieces, axis=0).astype(jnp.bfloat16)


def _sweep(g_ref, src_ref, valid, span, rows, blocks):
    full = (span - 1) // 8

    def group(q, acc):
        base = pl.multiple_of(q * 8, 8)
        part = src_ref[pl.ds(base, rows + 8), :]
        taps = g_ref[0, pl.ds(base, 8), :]
        for r in range(8):
            t = _toeplitz(taps[r : r + 1], valid)
            acc = acc + jnp.dot(_lhs(part, r, rows, blocks), t, preferred_element_type=jnp.float32)
        return acc

    acc = lax.fori_loop(0, full, group, jnp.zeros((rows * blocks, LANES), jnp.float32))
    tail = span - 8 * full
    part = src_ref[pl.ds(8 * full, rows + tail - 1), :]
    taps = g_ref[0, pl.ds(8 * full, tail), :]
    for r in range(tail):
        t = _toeplitz(taps[r : r + 1], valid)
        acc = acc + jnp.dot(_lhs(part, r, rows, blocks), t, preferred_element_type=jnp.float32)
    return acc


def _blur_body(g_ref, x_ref, o_ref, *, span, rows, blocks):
    k = pl.program_id(0)

    @pl.when(k == 0)
    def _():
        o_ref[...] = jnp.zeros_like(o_ref)

    valid = _band(span)
    acc = _sweep(g_ref, x_ref.at[0], valid, span, rows, blocks)
    o_ref[...] += acc


def blur(g, x, rows):
    nk, span, _ = g.shape
    src_rows, padded_width = x.shape[1], x.shape[2]
    blocks = (padded_width - LANES) // LANES
    out = pl.pallas_call(
        functools.partial(_blur_body, span=span, rows=rows, blocks=blocks),
        grid=(nk,),
        in_specs=[
            pl.BlockSpec((1, span, LANES), lambda k: (k, 0, 0)),
            pl.BlockSpec((1, src_rows, padded_width), lambda k: (k, 0, 0)),
        ],
        out_specs=pl.BlockSpec((rows * blocks, LANES), lambda k: (0, 0)),
        out_shape=jax.ShapeDtypeStruct((rows * blocks, LANES), jnp.float32),
        compiler_params=pltpu.CompilerParams(dimension_semantics=("arbitrary",)),
    )(g, x)
    return jnp.concatenate([out[n * rows : (n + 1) * rows] for n in range(blocks)], axis=1)


def _back_body(g_ref, e_ref, w_ref, o_ref, *, span, rows, blocks):
    k = pl.program_id(0)

    @pl.when(k == 0)
    def _():
        o_ref[...] = jnp.zeros_like(o_ref)

    valid = _band(span)

    acc = _sweep(g_ref, e_ref, valid, span, rows, blocks)
    for n in range(blocks):
        cols = slice(n * LANES, (n + 1) * LANES)
        w = w_ref[0, :, cols].astype(jnp.float32)
        o_ref[:, cols] += w * acc[n * rows : (n + 1) * rows]


def back_weighted(g, e, w):
    nk, span, _ = g.shape
    rows, width = w.shape[1], w.shape[2]
    blocks = width // LANES
    return pl.pallas_call(
        functools.partial(_back_body, span=span, rows=rows, blocks=blocks),
        grid=(nk,),
        in_specs=[
            pl.BlockSpec((1, span, LANES), lambda k: (k, 0, 0)),
            pl.BlockSpec(e.shape, lambda k: (0, 0)),
            pl.BlockSpec((1, rows, width), lambda k: (k, 0, 0)),
        ],
        out_specs=pl.BlockSpec((rows, width), lambda k: (0, 0)),
        out_shape=jax.ShapeDtypeStruct((rows, width), jnp.float32),
        compiler_params=pltpu.CompilerParams(dimension_semantics=("arbitrary",)),
    )(g, e, w)


def per_device(
    estimate, residual, direction, kernels, weight_maps, filters_in, biases, filters_out
):
    rows, width = direction.shape
    half = (kernels.shape[1] - 1) // 2
    maps_wide = weight_maps.astype(jnp.float32)
    shaped = (maps_wide * direction[None]).astype(jnp.bfloat16)
    padded = with_halo(shaped, (("band", 1),), half)
    framed = jnp.pad(padded.astype(jnp.float32), ((0, 0), (0, 0), (half, LANES - half)))
    partial_value = blur(tap_rows(kernels), framed, rows)
    image = lax.psum(partial_value, "comp").astype(jnp.bfloat16)
    edged = with_halo(image, (("band", 0),), half)
    edged = jnp.pad(edged.astype(jnp.float32), ((0, 0), (half, LANES - half)))
    local_sum = back_weighted(tap_rows(kernels[:, ::-1, ::-1]), edged, weight_maps)
    normal = lax.psum(local_sum, "comp")
    curved = normal + damping * direction
    old, product, cross, square = lax.psum(
        (
            jnp.sum(residual * residual),
            jnp.sum(direction * curved),
            jnp.sum(residual * curved),
            jnp.sum(curved * curved),
        ),
        "band",
    )
    alpha = old / product
    residual_next = residual - alpha * curved
    new = old - 2.0 * alpha * cross + alpha * alpha * square
    estimate_next = estimate + alpha * direction
    direction_next = residual_next + new / old * direction
    denoised = denoise(estimate_next, filters_in, biases, filters_out)
    return (estimate_next, residual_next, direction_next, denoised)


def solution(mesh):
    return jax.shard_map(
        per_device,
        mesh=mesh,
        in_specs=(
            P("band", None),
            P("band", None),
            P("band", None),
            P("comp", None, None),
            P("comp", "band", None),
            P(),
            P(),
            P(),
        ),
        out_specs=(P("band", None), P("band", None), P("band", None), P("band", "comp")),
        check_vma=False,
    )
```

```python
import functools

import jax
import jax.numpy as jnp
from jax import lax
from jax.experimental import pallas as pl
from jax.experimental.pallas import tpu as pltpu
from jax.sharding import PartitionSpec as P

damping = 0.5
LANES = 128


def with_halo(array, sides, width):
    for axis, dim in sides:
        count, length = (lax.axis_size(axis), array.shape[dim])
        up = [(i, (i + 1) % count) for i in range(count - 1)]
        down = [(j, i) for i, j in up]
        last = lax.slice_in_dim(array, length - width, length, axis=dim)
        first = lax.slice_in_dim(array, 0, width, axis=dim)
        before = lax.ppermute(last, axis, up)
        after = lax.ppermute(first, axis, down)
        array = jnp.concatenate([before, array, after], axis=dim)
    return array


def pair_sum(value, axis):
    count = lax.axis_size(axis)
    step = 1
    while step < count:
        value = value + lax.ppermute(value, axis, [(i, i ^ step) for i in range(count)])
        step *= 2
    return value


def denoise(framed, filters_in, biases, filters_out):
    rows, width = framed.shape[0] - 4, framed.shape[1]
    columns = width // lax.axis_size("comp")
    start = lax.axis_index("comp") * columns
    padded = jnp.pad(framed, ((0, 0), (2, 2)))
    tile = lax.dynamic_slice_in_dim(padded, start, columns + 4, 1)
    taps = jnp.stack(
        [tile[a : a + rows + 2, b : b + columns + 2] for a in range(3) for b in range(3)]
    )
    channels = filters_in.shape[0]
    features = jnp.einsum(
        "ct,tij->cij", filters_in.reshape(channels, 9), taps, precision=lax.Precision.HIGHEST
    )
    features = jax.nn.relu(features + biases[:, None, None])
    total_rows = rows * lax.axis_size("band")
    global_rows = lax.axis_index("band") * rows - 1 + jnp.arange(rows + 2)
    global_cols = start - 1 + jnp.arange(columns + 2)
    inside_rows = (global_rows >= 0) & (global_rows < total_rows)
    inside_cols = (global_cols >= 0) & (global_cols < width)
    inside = (inside_rows[:, None] & inside_cols[None, :]).astype(jnp.float32)
    features = features * inside[None]
    spread = jnp.einsum(
        "ct,cij->tij", filters_out.reshape(channels, 9), features, precision=lax.Precision.HIGHEST
    )
    mixed = sum(
        (spread[a * 3 + b, a : a + rows, b : b + columns] for a in range(3) for b in range(3))
    )
    return tile[2 : 2 + rows, 2 : 2 + columns] - mixed


def tap_rows(kernels):
    span = kernels.shape[2]
    idx = (LANES - jnp.arange(LANES)) % LANES
    taps = kernels.astype(jnp.float32)[:, :, jnp.clip(idx, 0, span - 1)]
    return jnp.where((idx < span)[None, None], taps, 0.0)


def _toeplitz(g, valid):
    t = pltpu.roll(jnp.broadcast_to(g, valid.shape), 0, 1, stride=1, stride_axis=0)
    return jnp.where(valid, t, 0.0).astype(jnp.bfloat16)


def _band(span):
    p = lax.broadcasted_iota(jnp.int32, (2 * LANES, LANES), 0)
    v = lax.broadcasted_iota(jnp.int32, (2 * LANES, LANES), 1)
    d = p - v
    return (d >= 0) & (d < span)


def _lhs(part, r, rows, blocks):
    pieces = [part[r : r + rows, n * LANES : n * LANES + 2 * LANES] for n in range(blocks)]
    return jnp.concatenate(pieces, axis=0).astype(jnp.bfloat16)


def _sweep(g_ref, src_ref, valid, span, rows, blocks):
    full = (span - 1) // 8

    def group(q, acc):
        base = pl.multiple_of(q * 8, 8)
        part = src_ref[pl.ds(base, rows + 8), :]
        taps = g_ref[0, pl.ds(base, 8), :]
        for r in range(8):
            t = _toeplitz(taps[r : r + 1], valid)
            acc = acc + jnp.dot(_lhs(part, r, rows, blocks), t, preferred_element_type=jnp.float32)
        return acc

    acc = lax.fori_loop(0, full, group, jnp.zeros((rows * blocks, LANES), jnp.float32))
    tail = span - 8 * full
    part = src_ref[pl.ds(8 * full, rows + tail - 1), :]
    taps = g_ref[0, pl.ds(8 * full, tail), :]
    for r in range(tail):
        t = _toeplitz(taps[r : r + 1], valid)
        acc = acc + jnp.dot(_lhs(part, r, rows, blocks), t, preferred_element_type=jnp.float32)
    return acc


def _blur_body(g_ref, x_ref, o_ref, *, span, rows, blocks):
    k = pl.program_id(0)

    @pl.when(k == 0)
    def _():
        o_ref[...] = jnp.zeros_like(o_ref)

    valid = _band(span)
    acc = _sweep(g_ref, x_ref.at[0], valid, span, rows, blocks)
    o_ref[...] += acc


def blur(g, x, rows):
    nk, span, _ = g.shape
    src_rows, padded_width = x.shape[1], x.shape[2]
    blocks = (padded_width - LANES) // LANES
    out = pl.pallas_call(
        functools.partial(_blur_body, span=span, rows=rows, blocks=blocks),
        grid=(nk,),
        in_specs=[
            pl.BlockSpec((1, span, LANES), lambda k: (k, 0, 0)),
            pl.BlockSpec((1, src_rows, padded_width), lambda k: (k, 0, 0)),
        ],
        out_specs=pl.BlockSpec((rows * blocks, LANES), lambda k: (0, 0)),
        out_shape=jax.ShapeDtypeStruct((rows * blocks, LANES), jnp.float32),
        compiler_params=pltpu.CompilerParams(dimension_semantics=("arbitrary",)),
    )(g, x)
    return jnp.concatenate([out[n * rows : (n + 1) * rows] for n in range(blocks)], axis=1)


def _back_body(g_ref, e_ref, w_ref, o_ref, *, span, rows, blocks):
    k = pl.program_id(0)

    @pl.when(k == 0)
    def _():
        o_ref[...] = jnp.zeros_like(o_ref)

    valid = _band(span)

    acc = _sweep(g_ref, e_ref, valid, span, rows, blocks)
    for n in range(blocks):
        cols = slice(n * LANES, (n + 1) * LANES)
        w = w_ref[0, :, cols].astype(jnp.float32)
        o_ref[:, cols] += w * acc[n * rows : (n + 1) * rows]


def back_weighted(g, e, w):
    nk, span, _ = g.shape
    rows, width = w.shape[1], w.shape[2]
    blocks = width // LANES
    return pl.pallas_call(
        functools.partial(_back_body, span=span, rows=rows, blocks=blocks),
        grid=(nk,),
        in_specs=[
            pl.BlockSpec((1, span, LANES), lambda k: (k, 0, 0)),
            pl.BlockSpec(e.shape, lambda k: (0, 0)),
            pl.BlockSpec((1, rows, width), lambda k: (k, 0, 0)),
        ],
        out_specs=pl.BlockSpec((rows, width), lambda k: (0, 0)),
        out_shape=jax.ShapeDtypeStruct((rows, width), jnp.float32),
        compiler_params=pltpu.CompilerParams(dimension_semantics=("arbitrary",)),
    )(g, e, w)


def per_device(
    estimate, residual, direction, kernels, weight_maps, filters_in, biases, filters_out
):
    rows, width = direction.shape
    half = (kernels.shape[1] - 1) // 2
    framed_both = with_halo(jnp.stack([estimate, direction]), (("band", 1),), 2)
    framed_estimate, framed_direction = framed_both[0], framed_both[1]
    maps_wide = weight_maps.astype(jnp.float32)
    shaped = (maps_wide * direction[None]).astype(jnp.bfloat16)
    padded = with_halo(shaped, (("band", 1),), half)
    framed = jnp.pad(padded.astype(jnp.float32), ((0, 0), (0, 0), (half, LANES - half)))
    partial_value = blur(tap_rows(kernels), framed, rows)
    image = lax.psum(partial_value, "comp").astype(jnp.bfloat16)
    edged = with_halo(image, (("band", 0),), half)
    edged = jnp.pad(edged.astype(jnp.float32), ((0, 0), (half, LANES - half)))
    local_sum = back_weighted(tap_rows(kernels[:, ::-1, ::-1]), edged, weight_maps)
    normal = pair_sum(local_sum, "comp")
    curved = normal + damping * direction
    old, product, cross, square = lax.psum(
        (
            jnp.sum(residual * residual),
            jnp.sum(direction * curved),
            jnp.sum(residual * curved),
            jnp.sum(curved * curved),
        ),
        "band",
    )
    alpha = old / product
    residual_next = residual - alpha * curved
    new = old - 2.0 * alpha * cross + alpha * alpha * square
    estimate_next = estimate + alpha * direction
    direction_next = residual_next + new / old * direction
    framed_next = framed_estimate + alpha * framed_direction
    framed_next = lax.dynamic_update_slice_in_dim(framed_next, estimate_next, 2, 0)
    denoised = denoise(framed_next, filters_in, biases, filters_out)
    return (estimate_next, residual_next, direction_next, denoised)


def solution(mesh):
    return jax.shard_map(
        per_device,
        mesh=mesh,
        in_specs=(
            P("band", None),
            P("band", None),
            P("band", None),
            P("comp", None, None),
            P("comp", "band", None),
            P(),
            P(),
            P(),
        ),
        out_specs=(P("band", None), P("band", None), P("band", None), P("band", "comp")),
        check_vma=False,
    )
```

```python
import functools

import jax
import jax.numpy as jnp
from jax import lax
from jax.experimental import pallas as pl
from jax.experimental.pallas import tpu as pltpu
from jax.sharding import PartitionSpec as P

damping = 0.5
LANES = 128
GROUP = 16


def with_halo(array, sides, width):
    for axis, dim in sides:
        count, length = (lax.axis_size(axis), array.shape[dim])
        up = [(i, (i + 1) % count) for i in range(count - 1)]
        down = [(j, i) for i, j in up]
        last = lax.slice_in_dim(array, length - width, length, axis=dim)
        first = lax.slice_in_dim(array, 0, width, axis=dim)
        before = lax.ppermute(last, axis, up)
        after = lax.ppermute(first, axis, down)
        array = jnp.concatenate([before, array, after], axis=dim)
    return array


def pair_sum(value, axis):
    count = lax.axis_size(axis)
    step = 1
    while step < count:
        value = value + lax.ppermute(value, axis, [(i, i ^ step) for i in range(count)])
        step *= 2
    return value


def denoise(framed, filters_in, biases, filters_out):
    rows, width = framed.shape[0] - 4, framed.shape[1]
    columns = width // lax.axis_size("comp")
    start = lax.axis_index("comp") * columns
    padded = jnp.pad(framed, ((0, 0), (2, 2)))
    tile = lax.dynamic_slice_in_dim(padded, start, columns + 4, 1)
    taps = jnp.stack(
        [tile[a : a + rows + 2, b : b + columns + 2] for a in range(3) for b in range(3)]
    )
    channels = filters_in.shape[0]
    features = jnp.einsum(
        "ct,tij->cij", filters_in.reshape(channels, 9), taps, precision=lax.Precision.HIGHEST
    )
    features = jax.nn.relu(features + biases[:, None, None])
    total_rows = rows * lax.axis_size("band")
    global_rows = lax.axis_index("band") * rows - 1 + jnp.arange(rows + 2)
    global_cols = start - 1 + jnp.arange(columns + 2)
    inside_rows = (global_rows >= 0) & (global_rows < total_rows)
    inside_cols = (global_cols >= 0) & (global_cols < width)
    inside = (inside_rows[:, None] & inside_cols[None, :]).astype(jnp.float32)
    features = features * inside[None]
    spread = jnp.einsum(
        "ct,cij->tij", filters_out.reshape(channels, 9), features, precision=lax.Precision.HIGHEST
    )
    mixed = sum(
        (spread[a * 3 + b, a : a + rows, b : b + columns] for a in range(3) for b in range(3))
    )
    return tile[2 : 2 + rows, 2 : 2 + columns] - mixed


def tap_rows(kernels):
    span = kernels.shape[2]
    idx = (LANES - jnp.arange(LANES)) % LANES
    taps = kernels.astype(jnp.float32)[:, :, jnp.clip(idx, 0, span - 1)]
    return jnp.where((idx < span)[None, None], taps, 0.0)


def _toeplitz(g, valid):
    t = pltpu.roll(jnp.broadcast_to(g, valid.shape), 0, 1, stride=1, stride_axis=0)
    return jnp.where(valid, t, 0.0).astype(jnp.bfloat16)


def _band(span):
    p = lax.broadcasted_iota(jnp.int32, (2 * LANES, LANES), 0)
    v = lax.broadcasted_iota(jnp.int32, (2 * LANES, LANES), 1)
    d = p - v
    return (d >= 0) & (d < span)


def _lhs(shifted_ref, r, base, rows, blocks):
    part = shifted_ref[r, pl.ds(base, rows), :]
    pieces = [part[:, n * LANES : n * LANES + 2 * LANES] for n in range(blocks)]
    return jnp.concatenate(pieces, axis=0)


def _shift_rows(src_ref, shifted_ref):
    src_rows = src_ref.shape[0]
    for r in range(GROUP):
        shifted_ref[r, 0 : src_rows - r, :] = src_ref[r:src_rows, :].astype(jnp.bfloat16)


def _sweep(g_ref, shifted_ref, valid, span, rows, blocks):
    full = (span - 1) // GROUP

    def group(q, acc):
        base = pl.multiple_of(q * GROUP, GROUP)
        taps = g_ref[0, pl.ds(base, GROUP), :]
        for r in range(GROUP):
            t = _toeplitz(taps[r : r + 1], valid)
            lhs = _lhs(shifted_ref, r, base, rows, blocks)
            acc = acc + jnp.dot(lhs, t, preferred_element_type=jnp.float32)
        return acc

    acc = lax.fori_loop(0, full, group, jnp.zeros((rows * blocks, LANES), jnp.float32))
    base = GROUP * full
    taps = g_ref[0, pl.ds(base, span - base), :]
    for r in range(span - base):
        t = _toeplitz(taps[r : r + 1], valid)
        acc = acc + jnp.dot(_lhs(shifted_ref, r, base, rows, blocks), t, preferred_element_type=jnp.float32)
    return acc


def _blur_body(g_ref, x_ref, o_ref, shifted_ref, *, span, rows, blocks):
    k = pl.program_id(0)

    @pl.when(k == 0)
    def _():
        o_ref[...] = jnp.zeros_like(o_ref)

    _shift_rows(x_ref.at[0], shifted_ref)
    acc = _sweep(g_ref, shifted_ref, _band(span), span, rows, blocks)
    o_ref[...] += acc


def blur(g, x, rows):
    nk, span, _ = g.shape
    src_rows, padded_width = x.shape[1], x.shape[2]
    blocks = (padded_width - LANES) // LANES
    out = pl.pallas_call(
        functools.partial(_blur_body, span=span, rows=rows, blocks=blocks),
        grid=(nk,),
        in_specs=[
            pl.BlockSpec((1, span, LANES), lambda k: (k, 0, 0)),
            pl.BlockSpec((1, src_rows, padded_width), lambda k: (k, 0, 0)),
        ],
        out_specs=pl.BlockSpec((rows * blocks, LANES), lambda k: (0, 0)),
        out_shape=jax.ShapeDtypeStruct((rows * blocks, LANES), jnp.float32),
        scratch_shapes=[pltpu.VMEM((GROUP, src_rows, padded_width), jnp.bfloat16)],
        compiler_params=pltpu.CompilerParams(dimension_semantics=("arbitrary",)),
    )(g, x)
    return jnp.concatenate([out[n * rows : (n + 1) * rows] for n in range(blocks)], axis=1)


def _back_body(g_ref, e_ref, w_ref, o_ref, shifted_ref, *, span, rows, blocks):
    k = pl.program_id(0)

    @pl.when(k == 0)
    def _():
        o_ref[...] = jnp.zeros_like(o_ref)
        _shift_rows(e_ref, shifted_ref)

    acc = _sweep(g_ref, shifted_ref, _band(span), span, rows, blocks)
    for n in range(blocks):
        cols = slice(n * LANES, (n + 1) * LANES)
        w = w_ref[0, :, cols].astype(jnp.float32)
        o_ref[:, cols] += w * acc[n * rows : (n + 1) * rows]


def back_weighted(g, e, w):
    nk, span, _ = g.shape
    rows, width = w.shape[1], w.shape[2]
    blocks = width // LANES
    return pl.pallas_call(
        functools.partial(_back_body, span=span, rows=rows, blocks=blocks),
        grid=(nk,),
        in_specs=[
            pl.BlockSpec((1, span, LANES), lambda k: (k, 0, 0)),
            pl.BlockSpec(e.shape, lambda k: (0, 0)),
            pl.BlockSpec((1, rows, width), lambda k: (k, 0, 0)),
        ],
        out_specs=pl.BlockSpec((rows, width), lambda k: (0, 0)),
        out_shape=jax.ShapeDtypeStruct((rows, width), jnp.float32),
        scratch_shapes=[pltpu.VMEM((GROUP,) + e.shape, jnp.bfloat16)],
        compiler_params=pltpu.CompilerParams(dimension_semantics=("arbitrary",)),
    )(g, e, w)


def per_device(
    estimate, residual, direction, kernels, weight_maps, filters_in, biases, filters_out
):
    rows, width = direction.shape
    half = (kernels.shape[1] - 1) // 2
    framed_both = with_halo(jnp.stack([estimate, direction]), (("band", 1),), 2)
    framed_estimate, framed_direction = framed_both[0], framed_both[1]
    maps_wide = weight_maps.astype(jnp.float32)
    shaped = (maps_wide * direction[None]).astype(jnp.bfloat16)
    padded = with_halo(shaped, (("band", 1),), half)
    framed = jnp.pad(padded.astype(jnp.float32), ((0, 0), (0, 0), (half, LANES - half)))
    partial_value = blur(tap_rows(kernels), framed, rows)
    image = pair_sum(partial_value, "comp").astype(jnp.bfloat16)
    edged = with_halo(image, (("band", 0),), half)
    edged = jnp.pad(edged.astype(jnp.float32), ((0, 0), (half, LANES - half)))
    local_sum = back_weighted(tap_rows(kernels[:, ::-1, ::-1]), edged, weight_maps)
    normal = pair_sum(local_sum, "comp")
    curved = normal + damping * direction
    old, product, cross, square = lax.psum(
        (
            jnp.sum(residual * residual),
            jnp.sum(direction * curved),
            jnp.sum(residual * curved),
            jnp.sum(curved * curved),
        ),
        "band",
    )
    alpha = old / product
    residual_next = residual - alpha * curved
    new = old - 2.0 * alpha * cross + alpha * alpha * square
    estimate_next = estimate + alpha * direction
    direction_next = residual_next + new / old * direction
    framed_next = framed_estimate + alpha * framed_direction
    framed_next = lax.dynamic_update_slice_in_dim(framed_next, estimate_next, 2, 0)
    denoised = denoise(framed_next, filters_in, biases, filters_out)
    return (estimate_next, residual_next, direction_next, denoised)


def solution(mesh):
    return jax.shard_map(
        per_device,
        mesh=mesh,
        in_specs=(
            P("band", None),
            P("band", None),
            P("band", None),
            P("comp", None, None),
            P("comp", "band", None),
            P(),
            P(),
            P(),
        ),
        out_specs=(P("band", None), P("band", None), P("band", None), P("band", "comp")),
        check_vma=False,
    )
```

```python
import functools

import jax
import jax.numpy as jnp
from jax import lax
from jax.experimental import pallas as pl
from jax.experimental.pallas import tpu as pltpu
from jax.sharding import PartitionSpec as P

damping = 0.5
LANES = 128
GROUP = 16


def with_halo(array, sides, width):
    for axis, dim in sides:
        count, length = (lax.axis_size(axis), array.shape[dim])
        up = [(i, (i + 1) % count) for i in range(count - 1)]
        down = [(j, i) for i, j in up]
        last = lax.slice_in_dim(array, length - width, length, axis=dim)
        first = lax.slice_in_dim(array, 0, width, axis=dim)
        before = lax.ppermute(last, axis, up)
        after = lax.ppermute(first, axis, down)
        array = jnp.concatenate([before, array, after], axis=dim)
    return array


def split3(value):
    parts = []
    for _ in range(3):
        part = lax.reduce_precision(value, exponent_bits=8, mantissa_bits=7)
        parts.append(part.astype(jnp.bfloat16))
        value = value - part
    return jnp.stack(parts)


def join3(parts):
    parts = parts.astype(jnp.float32)
    return (parts[0] + parts[1]) + parts[2]


def band_halo(shaped, edges, half, reach):
    count, rows = lax.axis_size("band"), shaped.shape[1]
    up = [(i, i + 1) for i in range(count - 1)]
    down = [(j, i) for i, j in up]
    width = shaped.shape[2]

    def slab(shaped_rows, edge_rows):
        coded = split3(edge_rows).reshape(-1, width)
        coded = jnp.pad(coded, ((0, half - coded.shape[0]), (0, 0)))
        return jnp.concatenate([shaped_rows, coded[None]], axis=0)

    last = slab(shaped[:, rows - half :], edges[:, edges.shape[1] - reach :])
    first = slab(shaped[:, :half], edges[:, :reach])
    before = lax.ppermute(last, "band", up)
    after = lax.ppermute(first, "band", down)
    nk, count_parts = shaped.shape[0], 3 * edges.shape[0] * reach
    decode = lambda got: join3(got[nk, :count_parts].reshape(3, edges.shape[0], reach, width))
    padded = jnp.concatenate([before[:nk], shaped, after[:nk]], axis=1)
    return padded, decode(before), decode(after)


def pair_sum(value, axis):
    count = lax.axis_size(axis)
    step = 1
    while step < count:
        value = value + lax.ppermute(value, axis, [(i, i ^ step) for i in range(count)])
        step *= 2
    return value


def denoise(framed, filters_in, biases, filters_out):
    rows, width = framed.shape[0] - 4, framed.shape[1]
    columns = width // lax.axis_size("comp")
    start = lax.axis_index("comp") * columns
    padded = jnp.pad(framed, ((0, 0), (2, 2)))
    tile = lax.dynamic_slice_in_dim(padded, start, columns + 4, 1)
    taps = jnp.stack(
        [tile[a : a + rows + 2, b : b + columns + 2] for a in range(3) for b in range(3)]
    )
    channels = filters_in.shape[0]
    features = jnp.einsum(
        "ct,tij->cij", filters_in.reshape(channels, 9), taps, precision=lax.Precision.HIGHEST
    )
    features = jax.nn.relu(features + biases[:, None, None])
    total_rows = rows * lax.axis_size("band")
    global_rows = lax.axis_index("band") * rows - 1 + jnp.arange(rows + 2)
    global_cols = start - 1 + jnp.arange(columns + 2)
    inside_rows = (global_rows >= 0) & (global_rows < total_rows)
    inside_cols = (global_cols >= 0) & (global_cols < width)
    inside = (inside_rows[:, None] & inside_cols[None, :]).astype(jnp.float32)
    features = features * inside[None]
    spread = jnp.einsum(
        "ct,cij->tij", filters_out.reshape(channels, 9), features, precision=lax.Precision.HIGHEST
    )
    mixed = sum(
        (spread[a * 3 + b, a : a + rows, b : b + columns] for a in range(3) for b in range(3))
    )
    return tile[2 : 2 + rows, 2 : 2 + columns] - mixed


def tap_rows(kernels):
    span = kernels.shape[2]
    idx = (LANES - jnp.arange(LANES)) % LANES
    taps = kernels.astype(jnp.float32)[:, :, jnp.clip(idx, 0, span - 1)]
    return jnp.where((idx < span)[None, None], taps, 0.0)


def _toeplitz(g, valid):
    t = pltpu.roll(jnp.broadcast_to(g, valid.shape), 0, 1, stride=1, stride_axis=0)
    return jnp.where(valid, t, 0.0).astype(jnp.bfloat16)


def _band(span):
    p = lax.broadcasted_iota(jnp.int32, (2 * LANES, LANES), 0)
    v = lax.broadcasted_iota(jnp.int32, (2 * LANES, LANES), 1)
    d = p - v
    return (d >= 0) & (d < span)


def _lhs(shifted_ref, r, base, rows, blocks):
    part = shifted_ref[r, pl.ds(base, rows), :]
    pieces = [part[:, n * LANES : n * LANES + 2 * LANES] for n in range(blocks)]
    return jnp.concatenate(pieces, axis=0)


def _shift_rows(src_ref, shifted_ref):
    src_rows = src_ref.shape[0]
    for r in range(GROUP):
        shifted_ref[r, 0 : src_rows - r, :] = src_ref[r:src_rows, :].astype(jnp.bfloat16)


def _sweep(g_ref, shifted_ref, valid, span, rows, blocks):
    full = (span - 1) // GROUP

    def group(q, acc):
        base = pl.multiple_of(q * GROUP, GROUP)
        taps = g_ref[0, pl.ds(base, GROUP), :]
        for r in range(GROUP):
            t = _toeplitz(taps[r : r + 1], valid)
            lhs = _lhs(shifted_ref, r, base, rows, blocks)
            acc = acc + jnp.dot(lhs, t, preferred_element_type=jnp.float32)
        return acc

    acc = lax.fori_loop(0, full, group, jnp.zeros((rows * blocks, LANES), jnp.float32))
    base = GROUP * full
    taps = g_ref[0, pl.ds(base, span - base), :]
    for r in range(span - base):
        t = _toeplitz(taps[r : r + 1], valid)
        acc = acc + jnp.dot(_lhs(shifted_ref, r, base, rows, blocks), t, preferred_element_type=jnp.float32)
    return acc


def _blur_body(g_ref, x_ref, o_ref, shifted_ref, *, span, rows, blocks):
    k = pl.program_id(0)

    @pl.when(k == 0)
    def _():
        o_ref[...] = jnp.zeros_like(o_ref)

    _shift_rows(x_ref.at[0], shifted_ref)
    acc = _sweep(g_ref, shifted_ref, _band(span), span, rows, blocks)
    o_ref[...] += acc


def blur(g, x, rows):
    nk, span, _ = g.shape
    src_rows, padded_width = x.shape[1], x.shape[2]
    blocks = (padded_width - LANES) // LANES
    out = pl.pallas_call(
        functools.partial(_blur_body, span=span, rows=rows, blocks=blocks),
        grid=(nk,),
        in_specs=[
            pl.BlockSpec((1, span, LANES), lambda k: (k, 0, 0)),
            pl.BlockSpec((1, src_rows, padded_width), lambda k: (k, 0, 0)),
        ],
        out_specs=pl.BlockSpec((rows * blocks, LANES), lambda k: (0, 0)),
        out_shape=jax.ShapeDtypeStruct((rows * blocks, LANES), jnp.float32),
        scratch_shapes=[pltpu.VMEM((GROUP, src_rows, padded_width), jnp.bfloat16)],
        compiler_params=pltpu.CompilerParams(dimension_semantics=("arbitrary",)),
    )(g, x)
    return jnp.concatenate([out[n * rows : (n + 1) * rows] for n in range(blocks)], axis=1)


def _back_body(g_ref, e_ref, w_ref, o_ref, shifted_ref, *, span, rows, blocks):
    k = pl.program_id(0)

    @pl.when(k == 0)
    def _():
        o_ref[...] = jnp.zeros_like(o_ref)
        _shift_rows(e_ref, shifted_ref)

    acc = _sweep(g_ref, shifted_ref, _band(span), span, rows, blocks)
    for n in range(blocks):
        cols = slice(n * LANES, (n + 1) * LANES)
        w = w_ref[0, :, cols].astype(jnp.float32)
        o_ref[:, cols] += w * acc[n * rows : (n + 1) * rows]


def back_weighted(g, e, w):
    nk, span, _ = g.shape
    rows, width = w.shape[1], w.shape[2]
    blocks = width // LANES
    return pl.pallas_call(
        functools.partial(_back_body, span=span, rows=rows, blocks=blocks),
        grid=(nk,),
        in_specs=[
            pl.BlockSpec((1, span, LANES), lambda k: (k, 0, 0)),
            pl.BlockSpec(e.shape, lambda k: (0, 0)),
            pl.BlockSpec((1, rows, width), lambda k: (k, 0, 0)),
        ],
        out_specs=pl.BlockSpec((rows, width), lambda k: (0, 0)),
        out_shape=jax.ShapeDtypeStruct((rows, width), jnp.float32),
        scratch_shapes=[pltpu.VMEM((GROUP,) + e.shape, jnp.bfloat16)],
        compiler_params=pltpu.CompilerParams(dimension_semantics=("arbitrary",)),
    )(g, e, w)


def per_device(
    estimate, residual, direction, kernels, weight_maps, filters_in, biases, filters_out
):
    rows, width = direction.shape
    half = (kernels.shape[1] - 1) // 2
    maps_wide = weight_maps.astype(jnp.float32)
    shaped = (maps_wide * direction[None]).astype(jnp.bfloat16)
    edges = jnp.stack([estimate, direction])
    padded, edge_before, edge_after = band_halo(shaped, edges, half, 2)
    framed_both = jnp.concatenate([edge_before, edges, edge_after], axis=1)
    framed_estimate, framed_direction = framed_both[0], framed_both[1]
    framed = jnp.pad(padded.astype(jnp.float32), ((0, 0), (0, 0), (half, LANES - half)))
    partial_value = blur(tap_rows(kernels), framed, rows)
    image = pair_sum(partial_value, "comp").astype(jnp.bfloat16)
    edged = with_halo(image, (("band", 0),), half)
    edged = jnp.pad(edged.astype(jnp.float32), ((0, 0), (half, LANES - half)))
    local_sum = back_weighted(tap_rows(kernels[:, ::-1, ::-1]), edged, weight_maps)
    normal = pair_sum(local_sum, "comp")
    curved = normal + damping * direction
    sums = jnp.stack(
        [
            jnp.sum(residual * residual),
            jnp.sum(direction * curved),
            jnp.sum(residual * curved),
            jnp.sum(curved * curved),
        ]
    )
    sums = jnp.where(lax.axis_index("comp") == 0, sums, 0.0)
    old, product, cross, square = lax.psum(sums, ("comp", "band"))
    alpha = old / product
    residual_next = residual - alpha * curved
    new = old - 2.0 * alpha * cross + alpha * alpha * square
    estimate_next = estimate + alpha * direction
    direction_next = residual_next + new / old * direction
    framed_next = framed_estimate + alpha * framed_direction
    framed_next = lax.dynamic_update_slice_in_dim(framed_next, estimate_next, 2, 0)
    denoised = denoise(framed_next, filters_in, biases, filters_out)
    return (estimate_next, residual_next, direction_next, denoised)


def solution(mesh):
    return jax.shard_map(
        per_device,
        mesh=mesh,
        in_specs=(
            P("band", None),
            P("band", None),
            P("band", None),
            P("comp", None, None),
            P("comp", "band", None),
            P(),
            P(),
            P(),
        ),
        out_specs=(P("band", None), P("band", None), P("band", None), P("band", "comp")),
        check_vma=False,
    )
```

```python
import functools

import jax
import jax.numpy as jnp
from jax import lax
from jax.experimental import pallas as pl
from jax.experimental.pallas import tpu as pltpu
from jax.sharding import PartitionSpec as P

damping = 0.5
LANES = 128
GROUP = 16


def with_halo(array, sides, width):
    for axis, dim in sides:
        count, length = (lax.axis_size(axis), array.shape[dim])
        up = [(i, (i + 1) % count) for i in range(count - 1)]
        down = [(j, i) for i, j in up]
        last = lax.slice_in_dim(array, length - width, length, axis=dim)
        first = lax.slice_in_dim(array, 0, width, axis=dim)
        before = lax.ppermute(last, axis, up)
        after = lax.ppermute(first, axis, down)
        array = jnp.concatenate([before, array, after], axis=dim)
    return array


def split3(value):
    parts = []
    for _ in range(3):
        part = lax.reduce_precision(value, exponent_bits=8, mantissa_bits=7)
        parts.append(part.astype(jnp.bfloat16))
        value = value - part
    return jnp.stack(parts)


def join3(parts):
    parts = parts.astype(jnp.float32)
    return (parts[0] + parts[1]) + parts[2]


def band_halo(shaped, edges, half, reach):
    count, rows = lax.axis_size("band"), shaped.shape[1]
    up = [(i, i + 1) for i in range(count - 1)]
    down = [(j, i) for i, j in up]
    width = shaped.shape[2]

    def slab(shaped_rows, edge_rows):
        coded = split3(edge_rows).reshape(-1, width)
        coded = jnp.pad(coded, ((0, half - coded.shape[0]), (0, 0)))
        return jnp.concatenate([shaped_rows, coded[None]], axis=0)

    last = slab(shaped[:, rows - half :], edges[:, edges.shape[1] - reach :])
    first = slab(shaped[:, :half], edges[:, :reach])
    before = lax.ppermute(last, "band", up)
    after = lax.ppermute(first, "band", down)
    nk, count_parts = shaped.shape[0], 3 * edges.shape[0] * reach
    decode = lambda got: join3(got[nk, :count_parts].reshape(3, edges.shape[0], reach, width))
    padded = jnp.concatenate([before[:nk], shaped, after[:nk]], axis=1)
    return padded, decode(before), decode(after)


def pair_sum(value, axis):
    count = lax.axis_size(axis)
    step = 1
    while step < count:
        value = value + lax.ppermute(value, axis, [(i, i ^ step) for i in range(count)])
        step *= 2
    return value


def denoise(framed, filters_in, biases, filters_out):
    rows, width = framed.shape[0] - 4, framed.shape[1]
    columns = width // lax.axis_size("comp")
    start = lax.axis_index("comp") * columns
    padded = jnp.pad(framed, ((0, 0), (2, 2)))
    tile = lax.dynamic_slice_in_dim(padded, start, columns + 4, 1)
    taps = jnp.stack(
        [tile[a : a + rows + 2, b : b + columns + 2] for a in range(3) for b in range(3)]
    )
    channels = filters_in.shape[0]
    features = jnp.einsum(
        "ct,tij->cij", filters_in.reshape(channels, 9), taps, precision=lax.Precision.HIGHEST
    )
    features = jax.nn.relu(features + biases[:, None, None])
    total_rows = rows * lax.axis_size("band")
    global_rows = lax.axis_index("band") * rows - 1 + jnp.arange(rows + 2)
    global_cols = start - 1 + jnp.arange(columns + 2)
    inside_rows = (global_rows >= 0) & (global_rows < total_rows)
    inside_cols = (global_cols >= 0) & (global_cols < width)
    inside = (inside_rows[:, None] & inside_cols[None, :]).astype(jnp.float32)
    features = features * inside[None]
    spread = jnp.einsum(
        "ct,cij->tij", filters_out.reshape(channels, 9), features, precision=lax.Precision.HIGHEST
    )
    mixed = sum(
        (spread[a * 3 + b, a : a + rows, b : b + columns] for a in range(3) for b in range(3))
    )
    return tile[2 : 2 + rows, 2 : 2 + columns] - mixed


def tap_rows(kernels):
    span = kernels.shape[2]
    idx = (LANES - jnp.arange(LANES)) % LANES
    taps = kernels.astype(jnp.float32)[:, :, jnp.clip(idx, 0, span - 1)]
    return jnp.where((idx < span)[None, None], taps, 0.0)


def _toeplitz(g, valid):
    t = pltpu.roll(jnp.broadcast_to(g, valid.shape), 0, 1, stride=1, stride_axis=0)
    return jnp.where(valid, t, 0.0).astype(jnp.bfloat16)


def _band(span):
    p = lax.broadcasted_iota(jnp.int32, (2 * LANES, LANES), 0)
    v = lax.broadcasted_iota(jnp.int32, (2 * LANES, LANES), 1)
    d = p - v
    return (d >= 0) & (d < span)


def _lhs(shifted_ref, r, base, rows, blocks):
    part = shifted_ref[r, pl.ds(base, rows), :]
    pieces = [part[:, n * LANES : n * LANES + 2 * LANES] for n in range(blocks)]
    return jnp.concatenate(pieces, axis=0)


def _shift_rows(src_ref, shifted_ref):
    src_rows = src_ref.shape[0]
    for r in range(GROUP):
        shifted_ref[r, 0 : src_rows - r, :] = src_ref[r:src_rows, :].astype(jnp.bfloat16)


def _sweep(g_ref, shifted_ref, valid, span, rows, blocks):
    full = (span - 1) // GROUP

    def group(q, acc):
        base = pl.multiple_of(q * GROUP, GROUP)
        taps = g_ref[0, pl.ds(base, GROUP), :]
        for r in range(GROUP):
            t = _toeplitz(taps[r : r + 1], valid)
            lhs = _lhs(shifted_ref, r, base, rows, blocks)
            acc = acc + jnp.dot(lhs, t, preferred_element_type=jnp.float32)
        return acc

    acc = lax.fori_loop(0, full, group, jnp.zeros((rows * blocks, LANES), jnp.float32))
    base = GROUP * full
    taps = g_ref[0, pl.ds(base, span - base), :]
    for r in range(span - base):
        t = _toeplitz(taps[r : r + 1], valid)
        acc = acc + jnp.dot(_lhs(shifted_ref, r, base, rows, blocks), t, preferred_element_type=jnp.float32)
    return acc


def _blur_body(g_ref, x_ref, o_ref, shifted_ref, *, span, rows, blocks):
    k = pl.program_id(0)

    @pl.when(k == 0)
    def _():
        o_ref[...] = jnp.zeros_like(o_ref)

    _shift_rows(x_ref.at[0], shifted_ref)
    acc = _sweep(g_ref, shifted_ref, _band(span), span, rows, blocks)
    o_ref[...] += acc


def blur(g, x, rows):
    nk, span, _ = g.shape
    src_rows, padded_width = x.shape[1], x.shape[2]
    blocks = (padded_width - LANES) // LANES
    out = pl.pallas_call(
        functools.partial(_blur_body, span=span, rows=rows, blocks=blocks),
        grid=(nk,),
        in_specs=[
            pl.BlockSpec((1, span, LANES), lambda k: (k, 0, 0)),
            pl.BlockSpec((1, src_rows, padded_width), lambda k: (k, 0, 0)),
        ],
        out_specs=pl.BlockSpec((rows * blocks, LANES), lambda k: (0, 0)),
        out_shape=jax.ShapeDtypeStruct((rows * blocks, LANES), jnp.float32),
        scratch_shapes=[pltpu.VMEM((GROUP, src_rows, padded_width), jnp.bfloat16)],
        compiler_params=pltpu.CompilerParams(dimension_semantics=("arbitrary",)),
    )(g, x)
    return jnp.concatenate([out[n * rows : (n + 1) * rows] for n in range(blocks)], axis=1)


def _back_body(g_ref, e_ref, w_ref, o_ref, shifted_ref, *, span, rows, blocks):
    k = pl.program_id(0)

    @pl.when(k == 0)
    def _():
        o_ref[...] = jnp.zeros_like(o_ref)
        _shift_rows(e_ref, shifted_ref)

    acc = _sweep(g_ref, shifted_ref, _band(span), span, rows, blocks)
    for n in range(blocks):
        cols = slice(n * LANES, (n + 1) * LANES)
        w = w_ref[0, :, cols].astype(jnp.float32)
        o_ref[:, cols] += w * acc[n * rows : (n + 1) * rows]


def back_weighted(g, e, w):
    nk, span, _ = g.shape
    rows, width = w.shape[1], w.shape[2]
    blocks = width // LANES
    return pl.pallas_call(
        functools.partial(_back_body, span=span, rows=rows, blocks=blocks),
        grid=(nk,),
        in_specs=[
            pl.BlockSpec((1, span, LANES), lambda k: (k, 0, 0)),
            pl.BlockSpec(e.shape, lambda k: (0, 0)),
            pl.BlockSpec((1, rows, width), lambda k: (k, 0, 0)),
        ],
        out_specs=pl.BlockSpec((rows, width), lambda k: (0, 0)),
        out_shape=jax.ShapeDtypeStruct((rows, width), jnp.float32),
        scratch_shapes=[pltpu.VMEM((GROUP,) + e.shape, jnp.bfloat16)],
        compiler_params=pltpu.CompilerParams(dimension_semantics=("arbitrary",)),
    )(g, e, w)


def per_device(
    estimate, residual, direction, kernels, weight_maps, filters_in, biases, filters_out
):
    rows, width = direction.shape
    half = (kernels.shape[1] - 1) // 2
    maps_wide = weight_maps.astype(jnp.float32)
    shaped = (maps_wide * direction[None]).astype(jnp.bfloat16)
    edges = jnp.stack([estimate, direction])
    padded, edge_before, edge_after = band_halo(shaped, edges, half, 2)
    framed_both = jnp.concatenate([edge_before, edges, edge_after], axis=1)
    framed_estimate, framed_direction = framed_both[0], framed_both[1]
    framed = jnp.pad(padded.astype(jnp.float32), ((0, 0), (0, 0), (half, LANES - half)))
    partial_value = blur(tap_rows(kernels), framed, rows)
    image = pair_sum(partial_value, "comp").astype(jnp.bfloat16)
    edged = with_halo(image, (("band", 0),), half)
    edged = jnp.pad(edged.astype(jnp.float32), ((0, 0), (half, LANES - half)))
    local_sum = back_weighted(tap_rows(kernels[:, ::-1, ::-1]), edged, weight_maps)
    normal = pair_sum(local_sum, "comp")
    curved = normal + damping * direction
    sums = jnp.stack(
        [
            jnp.sum(residual * residual),
            jnp.sum(direction * curved),
            jnp.sum(residual * curved),
            jnp.sum(curved * curved),
        ]
    )
    old, product, cross, square = lax.psum(sums, "band")
    alpha = old / product
    residual_next = residual - alpha * curved
    new = old - 2.0 * alpha * cross + alpha * alpha * square
    estimate_next = estimate + alpha * direction
    direction_next = residual_next + new / old * direction
    framed_next = framed_estimate + alpha * framed_direction
    framed_next = lax.dynamic_update_slice_in_dim(framed_next, estimate_next, 2, 0)
    denoised = denoise(framed_next, filters_in, biases, filters_out)
    return (estimate_next, residual_next, direction_next, denoised)


def solution(mesh):
    return jax.shard_map(
        per_device,
        mesh=mesh,
        in_specs=(
            P("band", None),
            P("band", None),
            P("band", None),
            P("comp", None, None),
            P("comp", "band", None),
            P(),
            P(),
            P(),
        ),
        out_specs=(P("band", None), P("band", None), P("band", None), P("band", "comp")),
        check_vma=False,
    )
```

```python
import functools

import jax
import jax.numpy as jnp
from jax import lax
from jax.experimental import pallas as pl
from jax.experimental.pallas import tpu as pltpu
from jax.sharding import PartitionSpec as P

damping = 0.5
LANES = 128
GROUP = 16


def with_halo(array, sides, width):
    for axis, dim in sides:
        count, length = (lax.axis_size(axis), array.shape[dim])
        up = [(i, (i + 1) % count) for i in range(count - 1)]
        down = [(j, i) for i, j in up]
        last = lax.slice_in_dim(array, length - width, length, axis=dim)
        first = lax.slice_in_dim(array, 0, width, axis=dim)
        before = lax.ppermute(last, axis, up)
        after = lax.ppermute(first, axis, down)
        array = jnp.concatenate([before, array, after], axis=dim)
    return array


def split3(value):
    parts = []
    for _ in range(3):
        part = lax.reduce_precision(value, exponent_bits=8, mantissa_bits=7)
        parts.append(part.astype(jnp.bfloat16))
        value = value - part
    return jnp.stack(parts)


def join3(parts):
    parts = parts.astype(jnp.float32)
    return (parts[0] + parts[1]) + parts[2]


def band_halo(shaped, edges, half, reach):
    count, rows = lax.axis_size("band"), shaped.shape[1]
    up = [(i, i + 1) for i in range(count - 1)]
    down = [(j, i) for i, j in up]
    width = shaped.shape[2]

    def slab(shaped_rows, edge_rows):
        coded = split3(edge_rows).reshape(-1, width)
        coded = jnp.pad(coded, ((0, half - coded.shape[0]), (0, 0)))
        return jnp.concatenate([shaped_rows, coded[None]], axis=0)

    last = slab(shaped[:, rows - half :], edges[:, edges.shape[1] - reach :])
    first = slab(shaped[:, :half], edges[:, :reach])
    before = lax.ppermute(last, "band", up)
    after = lax.ppermute(first, "band", down)
    nk, count_parts = shaped.shape[0], 3 * edges.shape[0] * reach
    decode = lambda got: join3(got[nk, :count_parts].reshape(3, edges.shape[0], reach, width))
    padded = jnp.concatenate([before[:nk], shaped, after[:nk]], axis=1)
    return padded, decode(before), decode(after)


def pair_sum(value, axis):
    count = lax.axis_size(axis)
    step = 1
    while step < count:
        value = value + lax.ppermute(value, axis, [(i, i ^ step) for i in range(count)])
        step *= 2
    return value


def denoise(framed, filters_in, biases, filters_out):
    rows, width = framed.shape[0] - 4, framed.shape[1]
    columns = width // lax.axis_size("comp")
    start = lax.axis_index("comp") * columns
    padded = jnp.pad(framed, ((0, 0), (2, 2)))
    tile = lax.dynamic_slice_in_dim(padded, start, columns + 4, 1)
    taps = jnp.stack(
        [tile[a : a + rows + 2, b : b + columns + 2] for a in range(3) for b in range(3)]
    )
    channels = filters_in.shape[0]
    features = jnp.einsum(
        "ct,tij->cij", filters_in.reshape(channels, 9), taps, precision=lax.Precision.HIGHEST
    )
    features = jax.nn.relu(features + biases[:, None, None])
    total_rows = rows * lax.axis_size("band")
    global_rows = lax.axis_index("band") * rows - 1 + jnp.arange(rows + 2)
    global_cols = start - 1 + jnp.arange(columns + 2)
    inside_rows = (global_rows >= 0) & (global_rows < total_rows)
    inside_cols = (global_cols >= 0) & (global_cols < width)
    inside = (inside_rows[:, None] & inside_cols[None, :]).astype(jnp.float32)
    features = features * inside[None]
    spread = jnp.einsum(
        "ct,cij->tij", filters_out.reshape(channels, 9), features, precision=lax.Precision.HIGHEST
    )
    mixed = sum(
        (spread[a * 3 + b, a : a + rows, b : b + columns] for a in range(3) for b in range(3))
    )
    return tile[2 : 2 + rows, 2 : 2 + columns] - mixed


def tap_rows(kernels):
    span = kernels.shape[2]
    idx = (LANES - jnp.arange(LANES)) % LANES
    taps = kernels.astype(jnp.float32)[:, :, jnp.clip(idx, 0, span - 1)]
    return jnp.where((idx < span)[None, None], taps, 0.0)


def _toeplitz(g, valid):
    t = pltpu.roll(jnp.broadcast_to(g, valid.shape), 0, 1, stride=1, stride_axis=0)
    return jnp.where(valid, t, 0.0).astype(jnp.bfloat16)


def _band(span):
    p = lax.broadcasted_iota(jnp.int32, (2 * LANES, LANES), 0)
    v = lax.broadcasted_iota(jnp.int32, (2 * LANES, LANES), 1)
    d = p - v
    return (d >= 0) & (d < span)


def _lhs(shifted_ref, r, base, rows, blocks):
    part = shifted_ref[r, pl.ds(base, rows), :]
    pieces = [part[:, n * LANES : n * LANES + 2 * LANES] for n in range(blocks)]
    return jnp.concatenate(pieces, axis=0)


def _shift_rows(src_ref, shifted_ref):
    src_rows = src_ref.shape[0]
    for r in range(GROUP):
        shifted_ref[r, 0 : src_rows - r, :] = src_ref[r:src_rows, :].astype(jnp.bfloat16)


def _sweep(g_ref, shifted_ref, valid, span, rows, blocks):
    full = (span - 1) // GROUP

    def group(q, acc):
        base = pl.multiple_of(q * GROUP, GROUP)
        taps = g_ref[0, pl.ds(base, GROUP), :]
        for r in range(GROUP):
            t = _toeplitz(taps[r : r + 1], valid)
            lhs = _lhs(shifted_ref, r, base, rows, blocks)
            acc = acc + jnp.dot(lhs, t, preferred_element_type=jnp.float32)
        return acc

    acc = lax.fori_loop(0, full, group, jnp.zeros((rows * blocks, LANES), jnp.float32))
    base = GROUP * full
    taps = g_ref[0, pl.ds(base, span - base), :]
    for r in range(span - base):
        t = _toeplitz(taps[r : r + 1], valid)
        acc = acc + jnp.dot(_lhs(shifted_ref, r, base, rows, blocks), t, preferred_element_type=jnp.float32)
    return acc


def _blur_body(g_ref, x_ref, o_ref, shifted_ref, *, span, rows, blocks):
    k = pl.program_id(0)

    @pl.when(k == 0)
    def _():
        o_ref[...] = jnp.zeros_like(o_ref)

    _shift_rows(x_ref.at[0], shifted_ref)
    acc = _sweep(g_ref, shifted_ref, _band(span), span, rows, blocks)
    o_ref[...] += acc


def blur(g, x, rows):
    nk, span, _ = g.shape
    src_rows, padded_width = x.shape[1], x.shape[2]
    blocks = (padded_width - LANES) // LANES
    out = pl.pallas_call(
        functools.partial(_blur_body, span=span, rows=rows, blocks=blocks),
        grid=(nk,),
        in_specs=[
            pl.BlockSpec((1, span, LANES), lambda k: (k, 0, 0)),
            pl.BlockSpec((1, src_rows, padded_width), lambda k: (k, 0, 0)),
        ],
        out_specs=pl.BlockSpec((rows * blocks, LANES), lambda k: (0, 0)),
        out_shape=jax.ShapeDtypeStruct((rows * blocks, LANES), jnp.float32),
        scratch_shapes=[pltpu.VMEM((GROUP, src_rows, padded_width), jnp.bfloat16)],
        compiler_params=pltpu.CompilerParams(dimension_semantics=("arbitrary",)),
    )(g, x)
    return jnp.concatenate([out[n * rows : (n + 1) * rows] for n in range(blocks)], axis=1)


def _back_body(g_ref, e_ref, w_ref, o_ref, shifted_ref, acc_ref, *, span, rows, blocks):
    nk = g_ref.shape[0]
    _shift_rows(e_ref, shifted_ref)
    acc_ref[...] = jnp.zeros_like(acc_ref)
    valid = _band(span)

    def step(taps, r, base):
        t = jnp.concatenate([_toeplitz(taps[k, r : r + 1], valid) for k in range(nk)], axis=1)
        lhs = _lhs(shifted_ref, r, base, rows, blocks)
        acc_ref[...] += jnp.dot(lhs, t, preferred_element_type=jnp.float32)

    full = (span - 1) // GROUP

    def group(q, carry):
        base = pl.multiple_of(q * GROUP, GROUP)
        taps = g_ref[:, pl.ds(base, GROUP), :]
        for r in range(GROUP):
            step(taps, r, base)
        return carry

    lax.fori_loop(0, full, group, 0)
    base = GROUP * full
    taps = g_ref[:, pl.ds(base, span - base), :]
    for r in range(span - base):
        step(taps, r, base)
    total = jnp.zeros(o_ref.shape, jnp.float32)
    for k in range(nk):
        back = jnp.concatenate(
            [acc_ref[n * rows : (n + 1) * rows, k * LANES : (k + 1) * LANES] for n in range(blocks)], axis=1
        )
        total = total + w_ref[k].astype(jnp.float32) * back
    o_ref[...] = total


def back_weighted(g, e, w):
    nk, span, _ = g.shape
    rows, width = w.shape[1], w.shape[2]
    blocks = width // LANES
    return pl.pallas_call(
        functools.partial(_back_body, span=span, rows=rows, blocks=blocks),
        out_shape=jax.ShapeDtypeStruct((rows, width), jnp.float32),
        scratch_shapes=[
            pltpu.VMEM((GROUP,) + e.shape, jnp.bfloat16),
            pltpu.VMEM((rows * blocks, nk * LANES), jnp.float32),
        ],
    )(g, e, w)


def per_device(
    estimate, residual, direction, kernels, weight_maps, filters_in, biases, filters_out
):
    rows, width = direction.shape
    half = (kernels.shape[1] - 1) // 2
    maps_wide = weight_maps.astype(jnp.float32)
    shaped = (maps_wide * direction[None]).astype(jnp.bfloat16)
    edges = jnp.stack([estimate, direction])
    padded, edge_before, edge_after = band_halo(shaped, edges, half, 2)
    framed_both = jnp.concatenate([edge_before, edges, edge_after], axis=1)
    framed_estimate, framed_direction = framed_both[0], framed_both[1]
    framed = jnp.pad(padded.astype(jnp.float32), ((0, 0), (0, 0), (half, LANES - half)))
    partial_value = blur(tap_rows(kernels), framed, rows)
    image = pair_sum(partial_value, "comp").astype(jnp.bfloat16)
    edged = with_halo(image, (("band", 0),), half)
    edged = jnp.pad(edged.astype(jnp.float32), ((0, 0), (half, LANES - half)))
    local_sum = back_weighted(tap_rows(kernels[:, ::-1, ::-1]), edged, weight_maps)
    normal = pair_sum(local_sum, "comp")
    curved = normal + damping * direction
    sums = jnp.stack(
        [
            jnp.sum(residual * residual),
            jnp.sum(direction * curved),
            jnp.sum(residual * curved),
            jnp.sum(curved * curved),
        ]
    )
    old, product, cross, square = lax.psum(sums, "band")
    alpha = old / product
    residual_next = residual - alpha * curved
    new = old - 2.0 * alpha * cross + alpha * alpha * square
    estimate_next = estimate + alpha * direction
    direction_next = residual_next + new / old * direction
    framed_next = framed_estimate + alpha * framed_direction
    framed_next = lax.dynamic_update_slice_in_dim(framed_next, estimate_next, 2, 0)
    denoised = denoise(framed_next, filters_in, biases, filters_out)
    return (estimate_next, residual_next, direction_next, denoised)


def solution(mesh):
    return jax.shard_map(
        per_device,
        mesh=mesh,
        in_specs=(
            P("band", None),
            P("band", None),
            P("band", None),
            P("comp", None, None),
            P("comp", "band", None),
            P(),
            P(),
            P(),
        ),
        out_specs=(P("band", None), P("band", None), P("band", None), P("band", "comp")),
        check_vma=False,
    )
```

```python
import functools

import jax
import jax.numpy as jnp
from jax import lax
from jax.experimental import pallas as pl
from jax.experimental.pallas import tpu as pltpu
from jax.sharding import PartitionSpec as P

damping = 0.5
LANES = 128
GROUP = 16


def with_halo(array, sides, width):
    for axis, dim in sides:
        count, length = (lax.axis_size(axis), array.shape[dim])
        up = [(i, (i + 1) % count) for i in range(count - 1)]
        down = [(j, i) for i, j in up]
        last = lax.slice_in_dim(array, length - width, length, axis=dim)
        first = lax.slice_in_dim(array, 0, width, axis=dim)
        before = lax.ppermute(last, axis, up)
        after = lax.ppermute(first, axis, down)
        array = jnp.concatenate([before, array, after], axis=dim)
    return array


def split3(value):
    parts = []
    for _ in range(3):
        part = lax.reduce_precision(value, exponent_bits=8, mantissa_bits=7)
        parts.append(part.astype(jnp.bfloat16))
        value = value - part
    return jnp.stack(parts)


def join3(parts):
    parts = parts.astype(jnp.float32)
    return (parts[0] + parts[1]) + parts[2]


def band_halo(shaped, edges, half, reach):
    count, rows = lax.axis_size("band"), shaped.shape[1]
    up = [(i, i + 1) for i in range(count - 1)]
    down = [(j, i) for i, j in up]
    width = shaped.shape[2]

    def slab(shaped_rows, edge_rows):
        coded = split3(edge_rows).reshape(-1, width)
        coded = jnp.pad(coded, ((0, half - coded.shape[0]), (0, 0)))
        return jnp.concatenate([shaped_rows, coded[None]], axis=0)

    last = slab(shaped[:, rows - half :], edges[:, edges.shape[1] - reach :])
    first = slab(shaped[:, :half], edges[:, :reach])
    before = lax.ppermute(last, "band", up)
    after = lax.ppermute(first, "band", down)
    nk, count_parts = shaped.shape[0], 3 * edges.shape[0] * reach
    decode = lambda got: join3(got[nk, :count_parts].reshape(3, edges.shape[0], reach, width))
    padded = jnp.concatenate([before[:nk], shaped, after[:nk]], axis=1)
    return padded, decode(before), decode(after)


def pair_sum(value, axis):
    count = lax.axis_size(axis)
    step = 1
    while step < count:
        value = value + lax.ppermute(value, axis, [(i, i ^ step) for i in range(count)])
        step *= 2
    return value


def denoise(framed, filters_in, biases, filters_out):
    rows, width = framed.shape[0] - 4, framed.shape[1]
    columns = width // lax.axis_size("comp")
    start = lax.axis_index("comp") * columns
    padded = jnp.pad(framed, ((0, 0), (2, 2)))
    tile = lax.dynamic_slice_in_dim(padded, start, columns + 4, 1)
    taps = jnp.stack(
        [tile[a : a + rows + 2, b : b + columns + 2] for a in range(3) for b in range(3)]
    )
    channels = filters_in.shape[0]
    features = jnp.einsum(
        "ct,tij->cij", filters_in.reshape(channels, 9), taps, precision=lax.Precision.HIGHEST
    )
    features = jax.nn.relu(features + biases[:, None, None])
    total_rows = rows * lax.axis_size("band")
    global_rows = lax.axis_index("band") * rows - 1 + jnp.arange(rows + 2)
    global_cols = start - 1 + jnp.arange(columns + 2)
    inside_rows = (global_rows >= 0) & (global_rows < total_rows)
    inside_cols = (global_cols >= 0) & (global_cols < width)
    inside = (inside_rows[:, None] & inside_cols[None, :]).astype(jnp.float32)
    features = features * inside[None]
    spread = jnp.einsum(
        "ct,cij->tij", filters_out.reshape(channels, 9), features, precision=lax.Precision.HIGHEST
    )
    mixed = sum(
        (spread[a * 3 + b, a : a + rows, b : b + columns] for a in range(3) for b in range(3))
    )
    return tile[2 : 2 + rows, 2 : 2 + columns] - mixed


def tap_rows(kernels):
    span = kernels.shape[2]
    idx = (LANES - jnp.arange(LANES)) % LANES
    taps = kernels.astype(jnp.float32)[:, :, jnp.clip(idx, 0, span - 1)]
    return jnp.where((idx < span)[None, None], taps, 0.0)


def _toeplitz(g, valid):
    t = pltpu.roll(jnp.broadcast_to(g, valid.shape), 0, 1, stride=1, stride_axis=0)
    return jnp.where(valid, t, 0.0).astype(jnp.bfloat16)


def _band(span):
    p = lax.broadcasted_iota(jnp.int32, (2 * LANES, LANES), 0)
    v = lax.broadcasted_iota(jnp.int32, (2 * LANES, LANES), 1)
    d = p - v
    return (d >= 0) & (d < span)


def _lhs(shifted_ref, r, base, rows, blocks):
    part = shifted_ref[r, pl.ds(base, rows), :]
    pieces = [part[:, n * LANES : n * LANES + 2 * LANES] for n in range(blocks)]
    return jnp.concatenate(pieces, axis=0)


def _shift_rows(src_ref, shifted_ref):
    src_rows = src_ref.shape[0]
    for r in range(GROUP):
        shifted_ref[r, 0 : src_rows - r, :] = src_ref[r:src_rows, :].astype(jnp.bfloat16)


def _sweep(g_ref, shifted_ref, valid, span, rows, blocks):
    full = (span - 1) // GROUP

    def group(q, acc):
        base = pl.multiple_of(q * GROUP, GROUP)
        taps = g_ref[0, pl.ds(base, GROUP), :]
        for r in range(GROUP):
            t = _toeplitz(taps[r : r + 1], valid)
            lhs = _lhs(shifted_ref, r, base, rows, blocks)
            acc = acc + jnp.dot(lhs, t, preferred_element_type=jnp.float32)
        return acc

    acc = lax.fori_loop(0, full, group, jnp.zeros((rows * blocks, LANES), jnp.float32))
    base = GROUP * full
    taps = g_ref[0, pl.ds(base, span - base), :]
    for r in range(span - base):
        t = _toeplitz(taps[r : r + 1], valid)
        acc = acc + jnp.dot(_lhs(shifted_ref, r, base, rows, blocks), t, preferred_element_type=jnp.float32)
    return acc


def _blur_sweep(g_ref, shifted_ref, valid, span, rows, blocks):
    tall = rows + GROUP
    full = (span - 1) // GROUP

    def pair(taps, r, base, acc):
        t = jnp.concatenate([_toeplitz(taps[r : r + 1], valid), _toeplitz(taps[r + 1 : r + 2], valid)], axis=1)
        z = jnp.dot(_lhs(shifted_ref, r, base, tall, blocks), t, preferred_element_type=jnp.float32)
        pieces = [
            z[n * tall : n * tall + rows, :LANES] + z[n * tall + 1 : n * tall + 1 + rows, LANES:]
            for n in range(blocks)
        ]
        return acc + jnp.concatenate(pieces, axis=0)

    def group(q, acc):
        base = pl.multiple_of(q * GROUP, GROUP)
        taps = g_ref[0, pl.ds(base, GROUP), :]
        for r in range(0, GROUP, 2):
            acc = pair(taps, r, base, acc)
        return acc

    acc = lax.fori_loop(0, full, group, jnp.zeros((rows * blocks, LANES), jnp.float32))
    base = GROUP * full
    taps = g_ref[0, pl.ds(base, span - base), :]
    for r in range(span - base):
        t = _toeplitz(taps[r : r + 1], valid)
        acc = acc + jnp.dot(_lhs(shifted_ref, r, base, rows, blocks), t, preferred_element_type=jnp.float32)
    return acc


def _blur_body(g_ref, x_ref, o_ref, shifted_ref, *, span, rows, blocks):
    k = pl.program_id(0)

    @pl.when(k == 0)
    def _():
        o_ref[...] = jnp.zeros_like(o_ref)

    _shift_rows(x_ref.at[0], shifted_ref)
    acc = _blur_sweep(g_ref, shifted_ref, _band(span), span, rows, blocks)
    o_ref[...] += acc


def blur(g, x, rows):
    nk, span, _ = g.shape
    src_rows, padded_width = x.shape[1], x.shape[2]
    blocks = (padded_width - LANES) // LANES
    out = pl.pallas_call(
        functools.partial(_blur_body, span=span, rows=rows, blocks=blocks),
        grid=(nk,),
        in_specs=[
            pl.BlockSpec((1, span, LANES), lambda k: (k, 0, 0)),
            pl.BlockSpec((1, src_rows, padded_width), lambda k: (k, 0, 0)),
        ],
        out_specs=pl.BlockSpec((rows * blocks, LANES), lambda k: (0, 0)),
        out_shape=jax.ShapeDtypeStruct((rows * blocks, LANES), jnp.float32),
        scratch_shapes=[pltpu.VMEM((GROUP, src_rows, padded_width), jnp.bfloat16)],
        compiler_params=pltpu.CompilerParams(dimension_semantics=("arbitrary",)),
    )(g, x)
    return jnp.concatenate([out[n * rows : (n + 1) * rows] for n in range(blocks)], axis=1)


def _back_body(g_ref, e_ref, w_ref, o_ref, shifted_ref, acc_ref, *, span, rows, blocks):
    nk = g_ref.shape[0]
    _shift_rows(e_ref, shifted_ref)
    acc_ref[...] = jnp.zeros_like(acc_ref)
    valid = _band(span)

    def step(taps, r, base):
        t = jnp.concatenate([_toeplitz(taps[k, r : r + 1], valid) for k in range(nk)], axis=1)
        lhs = _lhs(shifted_ref, r, base, rows, blocks)
        acc_ref[...] += jnp.dot(lhs, t, preferred_element_type=jnp.float32)

    full = (span - 1) // GROUP

    def group(q, carry):
        base = pl.multiple_of(q * GROUP, GROUP)
        taps = g_ref[:, pl.ds(base, GROUP), :]
        for r in range(GROUP):
            step(taps, r, base)
        return carry

    lax.fori_loop(0, full, group, 0)
    base = GROUP * full
    taps = g_ref[:, pl.ds(base, span - base), :]
    for r in range(span - base):
        step(taps, r, base)
    total = jnp.zeros(o_ref.shape, jnp.float32)
    for k in range(nk):
        back = jnp.concatenate(
            [acc_ref[n * rows : (n + 1) * rows, k * LANES : (k + 1) * LANES] for n in range(blocks)], axis=1
        )
        total = total + w_ref[k].astype(jnp.float32) * back
    o_ref[...] = total


def back_weighted(g, e, w):
    nk, span, _ = g.shape
    rows, width = w.shape[1], w.shape[2]
    blocks = width // LANES
    return pl.pallas_call(
        functools.partial(_back_body, span=span, rows=rows, blocks=blocks),
        out_shape=jax.ShapeDtypeStruct((rows, width), jnp.float32),
        scratch_shapes=[
            pltpu.VMEM((GROUP,) + e.shape, jnp.bfloat16),
            pltpu.VMEM((rows * blocks, nk * LANES), jnp.float32),
        ],
    )(g, e, w)


def per_device(
    estimate, residual, direction, kernels, weight_maps, filters_in, biases, filters_out
):
    rows, width = direction.shape
    half = (kernels.shape[1] - 1) // 2
    maps_wide = weight_maps.astype(jnp.float32)
    shaped = (maps_wide * direction[None]).astype(jnp.bfloat16)
    edges = jnp.stack([estimate, direction])
    padded, edge_before, edge_after = band_halo(shaped, edges, half, 2)
    framed_both = jnp.concatenate([edge_before, edges, edge_after], axis=1)
    framed_estimate, framed_direction = framed_both[0], framed_both[1]
    framed = jnp.pad(padded.astype(jnp.float32), ((0, 0), (0, 0), (half, LANES - half)))
    partial_value = blur(tap_rows(kernels), framed, rows)
    image = pair_sum(partial_value, "comp").astype(jnp.bfloat16)
    edged = with_halo(image, (("band", 0),), half)
    edged = jnp.pad(edged.astype(jnp.float32), ((0, 0), (half, LANES - half)))
    local_sum = back_weighted(tap_rows(kernels[:, ::-1, ::-1]), edged, weight_maps)
    normal = pair_sum(local_sum, "comp")
    curved = normal + damping * direction
    sums = jnp.stack(
        [
            jnp.sum(residual * residual),
            jnp.sum(direction * curved),
            jnp.sum(residual * curved),
            jnp.sum(curved * curved),
        ]
    )
    old, product, cross, square = lax.psum(sums, "band")
    alpha = old / product
    residual_next = residual - alpha * curved
    new = old - 2.0 * alpha * cross + alpha * alpha * square
    estimate_next = estimate + alpha * direction
    direction_next = residual_next + new / old * direction
    framed_next = framed_estimate + alpha * framed_direction
    framed_next = lax.dynamic_update_slice_in_dim(framed_next, estimate_next, 2, 0)
    denoised = denoise(framed_next, filters_in, biases, filters_out)
    return (estimate_next, residual_next, direction_next, denoised)


def solution(mesh):
    return jax.shard_map(
        per_device,
        mesh=mesh,
        in_specs=(
            P("band", None),
            P("band", None),
            P("band", None),
            P("comp", None, None),
            P("comp", "band", None),
            P(),
            P(),
            P(),
        ),
        out_specs=(P("band", None), P("band", None), P("band", None), P("band", "comp")),
        check_vma=False,
    )
```

```python
import functools

import jax
import jax.numpy as jnp
from jax import lax
from jax.experimental import pallas as pl
from jax.experimental.pallas import tpu as pltpu
from jax.sharding import PartitionSpec as P

damping = 0.5
LANES = 128
GROUP = 16


def with_halo(array, sides, width):
    for axis, dim in sides:
        count, length = (lax.axis_size(axis), array.shape[dim])
        up = [(i, (i + 1) % count) for i in range(count - 1)]
        down = [(j, i) for i, j in up]
        last = lax.slice_in_dim(array, length - width, length, axis=dim)
        first = lax.slice_in_dim(array, 0, width, axis=dim)
        before = lax.ppermute(last, axis, up)
        after = lax.ppermute(first, axis, down)
        array = jnp.concatenate([before, array, after], axis=dim)
    return array


def split3(value):
    parts = []
    for _ in range(3):
        part = lax.reduce_precision(value, exponent_bits=8, mantissa_bits=7)
        parts.append(part.astype(jnp.bfloat16))
        value = value - part
    return jnp.stack(parts)


def join3(parts):
    parts = parts.astype(jnp.float32)
    return (parts[0] + parts[1]) + parts[2]


def band_halo(shaped, edges, half, reach):
    count, rows = lax.axis_size("band"), shaped.shape[1]
    up = [(i, i + 1) for i in range(count - 1)]
    down = [(j, i) for i, j in up]
    width = shaped.shape[2]

    def slab(shaped_rows, edge_rows):
        coded = split3(edge_rows).reshape(-1, width)
        coded = jnp.pad(coded, ((0, half - coded.shape[0]), (0, 0)))
        return jnp.concatenate([shaped_rows, coded[None]], axis=0)

    last = slab(shaped[:, rows - half :], edges[:, edges.shape[1] - reach :])
    first = slab(shaped[:, :half], edges[:, :reach])
    before = lax.ppermute(last, "band", up)
    after = lax.ppermute(first, "band", down)
    nk, count_parts = shaped.shape[0], 3 * edges.shape[0] * reach
    decode = lambda got: join3(got[nk, :count_parts].reshape(3, edges.shape[0], reach, width))
    padded = jnp.concatenate([before[:nk], shaped, after[:nk]], axis=1)
    return padded, decode(before), decode(after)


def pair_sum(value, axis):
    count = lax.axis_size(axis)
    step = 1
    while step < count:
        value = value + lax.ppermute(value, axis, [(i, i ^ step) for i in range(count)])
        step *= 2
    return value


def denoise(framed, filters_in, biases, filters_out):
    rows, width = framed.shape[0] - 4, framed.shape[1]
    columns = width // lax.axis_size("comp")
    start = lax.axis_index("comp") * columns
    padded = jnp.pad(framed, ((0, 0), (2, 2)))
    tile = lax.dynamic_slice_in_dim(padded, start, columns + 4, 1)
    taps = jnp.stack(
        [tile[a : a + rows + 2, b : b + columns + 2] for a in range(3) for b in range(3)]
    )
    channels = filters_in.shape[0]
    features = jnp.einsum(
        "ct,tij->cij", filters_in.reshape(channels, 9), taps, precision=lax.Precision.HIGHEST
    )
    features = jax.nn.relu(features + biases[:, None, None])
    total_rows = rows * lax.axis_size("band")
    global_rows = lax.axis_index("band") * rows - 1 + jnp.arange(rows + 2)
    global_cols = start - 1 + jnp.arange(columns + 2)
    inside_rows = (global_rows >= 0) & (global_rows < total_rows)
    inside_cols = (global_cols >= 0) & (global_cols < width)
    inside = (inside_rows[:, None] & inside_cols[None, :]).astype(jnp.float32)
    features = features * inside[None]
    spread = jnp.einsum(
        "ct,cij->tij", filters_out.reshape(channels, 9), features, precision=lax.Precision.HIGHEST
    )
    mixed = sum(
        (spread[a * 3 + b, a : a + rows, b : b + columns] for a in range(3) for b in range(3))
    )
    return tile[2 : 2 + rows, 2 : 2 + columns] - mixed


def tap_rows(kernels):
    span = kernels.shape[2]
    idx = (LANES - jnp.arange(LANES)) % LANES
    taps = kernels.astype(jnp.float32)[:, :, jnp.clip(idx, 0, span - 1)]
    return jnp.where((idx < span)[None, None], taps, 0.0)


def _toeplitz(g, valid):
    t = pltpu.roll(jnp.broadcast_to(g, valid.shape), 0, 1, stride=1, stride_axis=0)
    return jnp.where(valid, t, 0.0).astype(jnp.bfloat16)


def _band(span):
    p = lax.broadcasted_iota(jnp.int32, (2 * LANES, LANES), 0)
    v = lax.broadcasted_iota(jnp.int32, (2 * LANES, LANES), 1)
    d = p - v
    return (d >= 0) & (d < span)


def _lhs(shifted_ref, r, base, rows, blocks):
    part = shifted_ref[r, pl.ds(base, rows), :]
    pieces = [part[:, n * LANES : n * LANES + 2 * LANES] for n in range(blocks)]
    return jnp.concatenate(pieces, axis=0)


def _shift_rows(src_ref, shifted_ref):
    src_rows = src_ref.shape[0]
    for r in range(GROUP):
        shifted_ref[r, 0 : src_rows - r, :] = src_ref[r:src_rows, :].astype(jnp.bfloat16)


def _sweep(g_ref, shifted_ref, valid, span, rows, blocks):
    full = (span - 1) // GROUP

    def group(q, acc):
        base = pl.multiple_of(q * GROUP, GROUP)
        taps = g_ref[0, pl.ds(base, GROUP), :]
        for r in range(GROUP):
            t = _toeplitz(taps[r : r + 1], valid)
            lhs = _lhs(shifted_ref, r, base, rows, blocks)
            acc = acc + jnp.dot(lhs, t, preferred_element_type=jnp.float32)
        return acc

    acc = lax.fori_loop(0, full, group, jnp.zeros((rows * blocks, LANES), jnp.float32))
    base = GROUP * full
    taps = g_ref[0, pl.ds(base, span - base), :]
    for r in range(span - base):
        t = _toeplitz(taps[r : r + 1], valid)
        acc = acc + jnp.dot(_lhs(shifted_ref, r, base, rows, blocks), t, preferred_element_type=jnp.float32)
    return acc


def _blur_sweep(g_ref, shifted_ref, valid, span, rows, blocks):
    tall = rows + GROUP
    full = (span - 1) // GROUP

    def pair(taps, r, base, acc):
        t = jnp.concatenate([_toeplitz(taps[r : r + 1], valid), _toeplitz(taps[r + 1 : r + 2], valid)], axis=1)
        z = jnp.dot(_lhs(shifted_ref, r, base, tall, blocks), t, preferred_element_type=jnp.float32)
        pieces = [
            z[n * tall : n * tall + rows, :LANES] + z[n * tall + 1 : n * tall + 1 + rows, LANES:]
            for n in range(blocks)
        ]
        return acc + jnp.concatenate(pieces, axis=0)

    def group(q, acc):
        base = pl.multiple_of(q * GROUP, GROUP)
        taps = g_ref[0, pl.ds(base, GROUP), :]
        for r in range(0, GROUP, 2):
            acc = pair(taps, r, base, acc)
        return acc

    acc = lax.fori_loop(0, full, group, jnp.zeros((rows * blocks, LANES), jnp.float32))
    base = GROUP * full
    taps = g_ref[0, pl.ds(base, span - base), :]
    for r in range(span - base):
        t = _toeplitz(taps[r : r + 1], valid)
        acc = acc + jnp.dot(_lhs(shifted_ref, r, base, rows, blocks), t, preferred_element_type=jnp.float32)
    return acc


def _blur_body(g_ref, x_ref, o_ref, shifted_ref, *, span, rows, blocks):
    k = pl.program_id(0)

    @pl.when(k == 0)
    def _():
        o_ref[...] = jnp.zeros_like(o_ref)

    _shift_rows(x_ref.at[0], shifted_ref)
    acc = _blur_sweep(g_ref, shifted_ref, _band(span), span, rows, blocks)
    o_ref[...] += acc


def blur(g, x, rows):
    nk, span, _ = g.shape
    src_rows, padded_width = x.shape[1], x.shape[2]
    blocks = (padded_width - LANES) // LANES
    out = pl.pallas_call(
        functools.partial(_blur_body, span=span, rows=rows, blocks=blocks),
        grid=(nk,),
        in_specs=[
            pl.BlockSpec((1, span, LANES), lambda k: (k, 0, 0)),
            pl.BlockSpec((1, src_rows, padded_width), lambda k: (k, 0, 0)),
        ],
        out_specs=pl.BlockSpec((rows * blocks, LANES), lambda k: (0, 0)),
        out_shape=jax.ShapeDtypeStruct((rows * blocks, LANES), jnp.float32),
        scratch_shapes=[pltpu.VMEM((GROUP, src_rows, padded_width), jnp.bfloat16)],
        compiler_params=pltpu.CompilerParams(dimension_semantics=("arbitrary",)),
    )(g, x)
    return jnp.concatenate([out[n * rows : (n + 1) * rows] for n in range(blocks)], axis=1)


def _back_body(g_ref, e_ref, w_ref, o_ref, shifted_ref, acc_ref, *, span, rows, blocks):
    nk = g_ref.shape[0]
    _shift_rows(e_ref, shifted_ref)
    acc_ref[...] = jnp.zeros_like(acc_ref)
    valid = _band(span)

    def step(taps, r, base):
        t = jnp.concatenate([_toeplitz(taps[k, r : r + 1], valid) for k in range(nk)], axis=1)
        lhs = _lhs(shifted_ref, r, base, rows, blocks)
        acc_ref[...] += jnp.dot(lhs, t, preferred_element_type=jnp.float32)

    full = (span - 1) // GROUP

    def group(q, carry):
        base = pl.multiple_of(q * GROUP, GROUP)
        taps = g_ref[:, pl.ds(base, GROUP), :]
        for r in range(GROUP):
            step(taps, r, base)
        return carry

    lax.fori_loop(0, full, group, 0)
    base = GROUP * full
    taps = g_ref[:, pl.ds(base, span - base), :]
    for r in range(span - base):
        step(taps, r, base)
    total = jnp.zeros(o_ref.shape, jnp.float32)
    for k in range(nk):
        back = jnp.concatenate(
            [acc_ref[n * rows : (n + 1) * rows, k * LANES : (k + 1) * LANES] for n in range(blocks)], axis=1
        )
        total = total + w_ref[k].astype(jnp.float32) * back
    o_ref[...] = total


def back_weighted(g, e, w):
    nk, span, _ = g.shape
    rows, width = w.shape[1], w.shape[2]
    blocks = width // LANES
    return pl.pallas_call(
        functools.partial(_back_body, span=span, rows=rows, blocks=blocks),
        out_shape=jax.ShapeDtypeStruct((rows, width), jnp.float32),
        scratch_shapes=[
            pltpu.VMEM((GROUP,) + e.shape, jnp.bfloat16),
            pltpu.VMEM((rows * blocks, nk * LANES), jnp.float32),
        ],
    )(g, e, w)


def per_device(
    estimate, residual, direction, kernels, weight_maps, filters_in, biases, filters_out
):
    rows, width = direction.shape
    half = (kernels.shape[1] - 1) // 2
    maps_wide = weight_maps.astype(jnp.float32)
    shaped = (maps_wide * direction[None]).astype(jnp.bfloat16)
    edges = jnp.stack([estimate, direction])
    padded, edge_before, edge_after = band_halo(shaped, edges, half, 2)
    framed_both = jnp.concatenate([edge_before, edges, edge_after], axis=1)
    framed_estimate, framed_direction = framed_both[0], framed_both[1]
    framed = jnp.pad(padded.astype(jnp.float32), ((0, 0), (0, 0), (half, LANES - half)))
    partial_value = blur(tap_rows(kernels), framed, rows)
    image = pair_sum(partial_value, "comp").astype(jnp.bfloat16)
    edged = with_halo(image, (("band", 0),), half)
    edged = jnp.pad(edged.astype(jnp.float32), ((0, 0), (half, LANES - half)))
    local_sum = back_weighted(tap_rows(kernels[:, ::-1, ::-1]), edged, weight_maps)
    normal = pair_sum(local_sum, "comp")
    curved = normal + damping * direction
    old, product, cross, square = lax.psum(
        (
            jnp.sum(residual * residual),
            jnp.sum(direction * curved),
            jnp.sum(residual * curved),
            jnp.sum(curved * curved),
        ),
        "band",
    )
    alpha = old / product
    residual_next = residual - alpha * curved
    new = old - 2.0 * alpha * cross + alpha * alpha * square
    estimate_next = estimate + alpha * direction
    direction_next = residual_next + new / old * direction
    framed_next = framed_estimate + alpha * framed_direction
    framed_next = lax.dynamic_update_slice_in_dim(framed_next, estimate_next, 2, 0)
    denoised = denoise(framed_next, filters_in, biases, filters_out)
    return (estimate_next, residual_next, direction_next, denoised)


def solution(mesh):
    return jax.shard_map(
        per_device,
        mesh=mesh,
        in_specs=(
            P("band", None),
            P("band", None),
            P("band", None),
            P("comp", None, None),
            P("comp", "band", None),
            P(),
            P(),
            P(),
        ),
        out_specs=(P("band", None), P("band", None), P("band", None), P("band", "comp")),
        check_vma=False,
    )
```

```python
import functools

import jax
import jax.numpy as jnp
from jax import lax
from jax.experimental import pallas as pl
from jax.experimental.pallas import tpu as pltpu
from jax.sharding import PartitionSpec as P

damping = 0.5
LANES = 128
GROUP = 16


def with_halo(array, sides, width):
    for axis, dim in sides:
        count, length = (lax.axis_size(axis), array.shape[dim])
        up = [(i, (i + 1) % count) for i in range(count - 1)]
        down = [(j, i) for i, j in up]
        last = lax.slice_in_dim(array, length - width, length, axis=dim)
        first = lax.slice_in_dim(array, 0, width, axis=dim)
        before = lax.ppermute(last, axis, up)
        after = lax.ppermute(first, axis, down)
        array = jnp.concatenate([before, array, after], axis=dim)
    return array


def split3(value):
    parts = []
    for _ in range(3):
        part = lax.reduce_precision(value, exponent_bits=8, mantissa_bits=7)
        parts.append(part.astype(jnp.bfloat16))
        value = value - part
    return jnp.stack(parts)


def join3(parts):
    parts = parts.astype(jnp.float32)
    return (parts[0] + parts[1]) + parts[2]


def band_halo(shaped, edges, half, reach):
    count, rows = lax.axis_size("band"), shaped.shape[1]
    up = [(i, i + 1) for i in range(count - 1)]
    down = [(j, i) for i, j in up]
    width = shaped.shape[2]

    def slab(shaped_rows, edge_rows):
        coded = split3(edge_rows).reshape(-1, width)
        coded = jnp.pad(coded, ((0, half - coded.shape[0]), (0, 0)))
        return jnp.concatenate([shaped_rows, coded[None]], axis=0)

    last = slab(shaped[:, rows - half :], edges[:, edges.shape[1] - reach :])
    first = slab(shaped[:, :half], edges[:, :reach])
    before = lax.ppermute(last, "band", up)
    after = lax.ppermute(first, "band", down)
    nk, count_parts = shaped.shape[0], 3 * edges.shape[0] * reach
    decode = lambda got: join3(got[nk, :count_parts].reshape(3, edges.shape[0], reach, width))
    padded = jnp.concatenate([before[:nk], shaped, after[:nk]], axis=1)
    return padded, decode(before), decode(after)


def pair_sum(value, axis):
    count = lax.axis_size(axis)
    step = 1
    while step < count:
        value = value + lax.ppermute(value, axis, [(i, i ^ step) for i in range(count)])
        step *= 2
    return value


def denoise(framed, filters_in, biases, filters_out):
    rows, width = framed.shape[0] - 4, framed.shape[1]
    columns = width // lax.axis_size("comp")
    start = lax.axis_index("comp") * columns
    padded = jnp.pad(framed, ((0, 0), (2, 2)))
    tile = lax.dynamic_slice_in_dim(padded, start, columns + 4, 1)
    taps = jnp.stack(
        [tile[a : a + rows + 2, b : b + columns + 2] for a in range(3) for b in range(3)]
    )
    channels = filters_in.shape[0]
    features = jnp.einsum(
        "ct,tij->cij", filters_in.reshape(channels, 9), taps, precision=lax.Precision.HIGHEST
    )
    features = jax.nn.relu(features + biases[:, None, None])
    total_rows = rows * lax.axis_size("band")
    global_rows = lax.axis_index("band") * rows - 1 + jnp.arange(rows + 2)
    global_cols = start - 1 + jnp.arange(columns + 2)
    inside_rows = (global_rows >= 0) & (global_rows < total_rows)
    inside_cols = (global_cols >= 0) & (global_cols < width)
    inside = (inside_rows[:, None] & inside_cols[None, :]).astype(jnp.float32)
    features = features * inside[None]
    spread = jnp.einsum(
        "ct,cij->tij", filters_out.reshape(channels, 9), features, precision=lax.Precision.HIGHEST
    )
    mixed = sum(
        (spread[a * 3 + b, a : a + rows, b : b + columns] for a in range(3) for b in range(3))
    )
    return tile[2 : 2 + rows, 2 : 2 + columns] - mixed


def tap_rows(kernels):
    span = kernels.shape[2]
    idx = (LANES - jnp.arange(LANES)) % LANES
    taps = kernels.astype(jnp.float32)[:, :, jnp.clip(idx, 0, span - 1)]
    return jnp.where((idx < span)[None, None], taps, 0.0)


def _toeplitz(g, valid):
    t = pltpu.roll(jnp.broadcast_to(g, valid.shape), 0, 1, stride=1, stride_axis=0)
    return jnp.where(valid, t, 0.0).astype(jnp.bfloat16)


def _band(span):
    p = lax.broadcasted_iota(jnp.int32, (2 * LANES, LANES), 0)
    v = lax.broadcasted_iota(jnp.int32, (2 * LANES, LANES), 1)
    d = p - v
    return (d >= 0) & (d < span)


def _lhs(shifted_ref, r, base, rows, blocks):
    part = shifted_ref[r, pl.ds(base, rows), :]
    pieces = [part[:, n * LANES : n * LANES + 2 * LANES] for n in range(blocks)]
    return jnp.concatenate(pieces, axis=0)


def _shift_rows(src_ref, shifted_ref):
    src_rows = src_ref.shape[0]
    for r in range(GROUP):
        shifted_ref[r, 0 : src_rows - r, :] = src_ref[r:src_rows, :].astype(jnp.bfloat16)


def _sweep(g_ref, shifted_ref, valid, span, rows, blocks):
    full = (span - 1) // GROUP

    def group(q, acc):
        base = pl.multiple_of(q * GROUP, GROUP)
        taps = g_ref[0, pl.ds(base, GROUP), :]
        for r in range(GROUP):
            t = _toeplitz(taps[r : r + 1], valid)
            lhs = _lhs(shifted_ref, r, base, rows, blocks)
            acc = acc + jnp.dot(lhs, t, preferred_element_type=jnp.float32)
        return acc

    acc = lax.fori_loop(0, full, group, jnp.zeros((rows * blocks, LANES), jnp.float32))
    base = GROUP * full
    taps = g_ref[0, pl.ds(base, span - base), :]
    for r in range(span - base):
        t = _toeplitz(taps[r : r + 1], valid)
        acc = acc + jnp.dot(_lhs(shifted_ref, r, base, rows, blocks), t, preferred_element_type=jnp.float32)
    return acc


def _blur_sweep(g_ref, shifted_ref, valid, span, rows, blocks):
    tall = rows + GROUP
    full = (span - 1) // GROUP

    def pair(taps, r, base, acc):
        t = jnp.concatenate([_toeplitz(taps[r : r + 1], valid), _toeplitz(taps[r + 1 : r + 2], valid)], axis=1)
        z = jnp.dot(_lhs(shifted_ref, r, base, tall, blocks), t, preferred_element_type=jnp.float32)
        pieces = [
            z[n * tall : n * tall + rows, :LANES] + z[n * tall + 1 : n * tall + 1 + rows, LANES:]
            for n in range(blocks)
        ]
        return acc + jnp.concatenate(pieces, axis=0)

    def group(q, acc):
        base = pl.multiple_of(q * GROUP, GROUP)
        taps = g_ref[0, pl.ds(base, GROUP), :]
        for r in range(0, GROUP, 2):
            acc = pair(taps, r, base, acc)
        return acc

    acc = lax.fori_loop(0, full, group, jnp.zeros((rows * blocks, LANES), jnp.float32))
    base = GROUP * full
    taps = g_ref[0, pl.ds(base, span - base), :]
    for r in range(span - base):
        t = _toeplitz(taps[r : r + 1], valid)
        acc = acc + jnp.dot(_lhs(shifted_ref, r, base, rows, blocks), t, preferred_element_type=jnp.float32)
    return acc


def _blur_body(g_ref, x_ref, o_ref, shifted_ref, *, span, rows, blocks):
    k = pl.program_id(0)

    @pl.when(k == 0)
    def _():
        o_ref[...] = jnp.zeros_like(o_ref)

    _shift_rows(x_ref.at[0], shifted_ref)
    acc = _blur_sweep(g_ref, shifted_ref, _band(span), span, rows, blocks)
    o_ref[...] += acc


def blur(g, x, rows):
    nk, span, _ = g.shape
    src_rows, padded_width = x.shape[1], x.shape[2]
    blocks = (padded_width - LANES) // LANES
    out = pl.pallas_call(
        functools.partial(_blur_body, span=span, rows=rows, blocks=blocks),
        grid=(nk,),
        in_specs=[
            pl.BlockSpec((1, span, LANES), lambda k: (k, 0, 0)),
            pl.BlockSpec((1, src_rows, padded_width), lambda k: (k, 0, 0)),
        ],
        out_specs=pl.BlockSpec((rows * blocks, LANES), lambda k: (0, 0)),
        out_shape=jax.ShapeDtypeStruct((rows * blocks, LANES), jnp.float32),
        scratch_shapes=[pltpu.VMEM((GROUP, src_rows, padded_width), jnp.bfloat16)],
        compiler_params=pltpu.CompilerParams(dimension_semantics=("arbitrary",)),
    )(g, x)
    return jnp.concatenate([out[n * rows : (n + 1) * rows] for n in range(blocks)], axis=1)


def _back_body(g_ref, e_ref, w_ref, o_ref, shifted_ref, acc_ref, *, span, rows, blocks):
    nk = g_ref.shape[0]
    _shift_rows(e_ref, shifted_ref)
    acc_ref[...] = jnp.zeros_like(acc_ref)
    valid = _band(span)

    def step(taps, r, base):
        t = jnp.concatenate([_toeplitz(taps[k, r : r + 1], valid) for k in range(nk)], axis=1)
        lhs = _lhs(shifted_ref, r, base, rows, blocks)
        acc_ref[...] += jnp.dot(lhs, t, preferred_element_type=jnp.float32)

    full = (span - 1) // GROUP

    def group(q, carry):
        base = pl.multiple_of(q * GROUP, GROUP)
        taps = g_ref[:, pl.ds(base, GROUP), :]
        for r in range(GROUP):
            step(taps, r, base)
        return carry

    lax.fori_loop(0, full, group, 0)
    base = GROUP * full
    taps = g_ref[:, pl.ds(base, span - base), :]
    for r in range(span - base):
        step(taps, r, base)
    total = jnp.zeros(o_ref.shape, jnp.float32)
    for k in range(nk):
        back = jnp.concatenate(
            [acc_ref[n * rows : (n + 1) * rows, k * LANES : (k + 1) * LANES] for n in range(blocks)], axis=1
        )
        total = total + w_ref[k].astype(jnp.float32) * back
    o_ref[...] = total


def back_weighted(g, e, w):
    nk, span, _ = g.shape
    rows, width = w.shape[1], w.shape[2]
    blocks = width // LANES
    return pl.pallas_call(
        functools.partial(_back_body, span=span, rows=rows, blocks=blocks),
        out_shape=jax.ShapeDtypeStruct((rows, width), jnp.float32),
        scratch_shapes=[
            pltpu.VMEM((GROUP,) + e.shape, jnp.bfloat16),
            pltpu.VMEM((rows * blocks, nk * LANES), jnp.float32),
        ],
    )(g, e, w)


def per_device(
    estimate, residual, direction, kernels, weight_maps, filters_in, biases, filters_out
):
    rows, width = direction.shape
    half = (kernels.shape[1] - 1) // 2
    maps_wide = weight_maps.astype(jnp.float32)
    shaped = (maps_wide * direction[None]).astype(jnp.bfloat16)
    edges = jnp.stack([estimate, direction])
    padded, edge_before, edge_after = band_halo(shaped, edges, half, 2)
    framed_both = jnp.concatenate([edge_before, edges, edge_after], axis=1)
    framed_estimate, framed_direction = framed_both[0], framed_both[1]
    framed = jnp.pad(padded, ((0, 0), (0, 0), (half, LANES - half)))
    partial_value = blur(tap_rows(kernels), framed, rows)
    image = pair_sum(partial_value, "comp").astype(jnp.bfloat16)
    edged = with_halo(image, (("band", 0),), half)
    edged = jnp.pad(edged, ((0, 0), (half, LANES - half)))
    local_sum = back_weighted(tap_rows(kernels[:, ::-1, ::-1]), edged, weight_maps)
    normal = pair_sum(local_sum, "comp")
    curved = normal + damping * direction
    old, product, cross, square = lax.psum(
        (
            jnp.sum(residual * residual),
            jnp.sum(direction * curved),
            jnp.sum(residual * curved),
            jnp.sum(curved * curved),
        ),
        "band",
    )
    alpha = old / product
    residual_next = residual - alpha * curved
    new = old - 2.0 * alpha * cross + alpha * alpha * square
    estimate_next = estimate + alpha * direction
    direction_next = residual_next + new / old * direction
    framed_next = framed_estimate + alpha * framed_direction
    framed_next = lax.dynamic_update_slice_in_dim(framed_next, estimate_next, 2, 0)
    denoised = denoise(framed_next, filters_in, biases, filters_out)
    return (estimate_next, residual_next, direction_next, denoised)


def solution(mesh):
    return jax.shard_map(
        per_device,
        mesh=mesh,
        in_specs=(
            P("band", None),
            P("band", None),
            P("band", None),
            P("comp", None, None),
            P("comp", "band", None),
            P(),
            P(),
            P(),
        ),
        out_specs=(P("band", None), P("band", None), P("band", None), P("band", "comp")),
        check_vma=False,
    )
```

```python
import functools

import jax
import jax.numpy as jnp
from jax import lax
from jax.experimental import pallas as pl
from jax.experimental.pallas import tpu as pltpu
from jax.sharding import PartitionSpec as P

damping = 0.5
LANES = 128
GROUP = 16


def with_halo(array, sides, width):
    for axis, dim in sides:
        count, length = (lax.axis_size(axis), array.shape[dim])
        up = [(i, (i + 1) % count) for i in range(count - 1)]
        down = [(j, i) for i, j in up]
        last = lax.slice_in_dim(array, length - width, length, axis=dim)
        first = lax.slice_in_dim(array, 0, width, axis=dim)
        before = lax.ppermute(last, axis, up)
        after = lax.ppermute(first, axis, down)
        array = jnp.concatenate([before, array, after], axis=dim)
    return array


def split3(value):
    parts = []
    for _ in range(3):
        part = lax.reduce_precision(value, exponent_bits=8, mantissa_bits=7)
        parts.append(part.astype(jnp.bfloat16))
        value = value - part
    return jnp.stack(parts)


def join3(parts):
    parts = parts.astype(jnp.float32)
    return (parts[0] + parts[1]) + parts[2]


def band_halo(shaped, edges, half, reach):
    count, rows = lax.axis_size("band"), shaped.shape[1]
    up = [(i, i + 1) for i in range(count - 1)]
    down = [(j, i) for i, j in up]
    width = shaped.shape[2]

    def slab(shaped_rows, edge_rows):
        coded = split3(edge_rows).reshape(-1, width)
        coded = jnp.pad(coded, ((0, half - coded.shape[0]), (0, 0)))
        return jnp.concatenate([shaped_rows, coded[None]], axis=0)

    last = slab(shaped[:, rows - half :], edges[:, edges.shape[1] - reach :])
    first = slab(shaped[:, :half], edges[:, :reach])
    before = lax.ppermute(last, "band", up)
    after = lax.ppermute(first, "band", down)
    nk, count_parts = shaped.shape[0], 3 * edges.shape[0] * reach
    decode = lambda got: join3(got[nk, :count_parts].reshape(3, edges.shape[0], reach, width))
    padded = jnp.concatenate([before[:nk], shaped, after[:nk]], axis=1)
    return padded, decode(before), decode(after)


def pair_sum(value, axis):
    count = lax.axis_size(axis)
    step = 1
    while step < count:
        value = value + lax.ppermute(value, axis, [(i, i ^ step) for i in range(count)])
        step *= 2
    return value


def denoise(framed, filters_in, biases, filters_out):
    rows, width = framed.shape[0] - 4, framed.shape[1]
    columns = width // lax.axis_size("comp")
    start = lax.axis_index("comp") * columns
    padded = jnp.pad(framed, ((0, 0), (2, 2)))
    tile = lax.dynamic_slice_in_dim(padded, start, columns + 4, 1)
    taps = jnp.stack(
        [tile[a : a + rows + 2, b : b + columns + 2] for a in range(3) for b in range(3)]
    )
    channels = filters_in.shape[0]
    features = jnp.einsum(
        "ct,tij->cij", filters_in.reshape(channels, 9), taps, precision=lax.Precision.HIGHEST
    )
    features = jax.nn.relu(features + biases[:, None, None])
    total_rows = rows * lax.axis_size("band")
    global_rows = lax.axis_index("band") * rows - 1 + jnp.arange(rows + 2)
    global_cols = start - 1 + jnp.arange(columns + 2)
    inside_rows = (global_rows >= 0) & (global_rows < total_rows)
    inside_cols = (global_cols >= 0) & (global_cols < width)
    inside = (inside_rows[:, None] & inside_cols[None, :]).astype(jnp.float32)
    features = features * inside[None]
    spread = jnp.einsum(
        "ct,cij->tij", filters_out.reshape(channels, 9), features, precision=lax.Precision.HIGHEST
    )
    mixed = sum(
        (spread[a * 3 + b, a : a + rows, b : b + columns] for a in range(3) for b in range(3))
    )
    return tile[2 : 2 + rows, 2 : 2 + columns] - mixed


def tap_rows(kernels):
    span = kernels.shape[2]
    idx = (LANES - jnp.arange(LANES)) % LANES
    taps = kernels.astype(jnp.float32)[:, :, jnp.clip(idx, 0, span - 1)]
    return jnp.where((idx < span)[None, None], taps, 0.0)


def _toeplitz(g, valid):
    t = pltpu.roll(jnp.broadcast_to(g, valid.shape), 0, 1, stride=1, stride_axis=0)
    return jnp.where(valid, t, 0.0).astype(jnp.bfloat16)


def _band(span):
    p = lax.broadcasted_iota(jnp.int32, (2 * LANES, LANES), 0)
    v = lax.broadcasted_iota(jnp.int32, (2 * LANES, LANES), 1)
    d = p - v
    return (d >= 0) & (d < span)


def _lhs(shifted_ref, r, base, rows, blocks):
    part = shifted_ref[r, pl.ds(base, rows), :]
    pieces = [part[:, n * LANES : n * LANES + 2 * LANES] for n in range(blocks)]
    return jnp.concatenate(pieces, axis=0)


def _shift_rows(src_ref, shifted_ref):
    src_rows = src_ref.shape[0]
    for r in range(GROUP):
        shifted_ref[r, 0 : src_rows - r, :] = src_ref[r:src_rows, :].astype(jnp.bfloat16)


def _sweep(g_ref, shifted_ref, valid, span, rows, blocks):
    full = (span - 1) // GROUP

    def group(q, acc):
        base = pl.multiple_of(q * GROUP, GROUP)
        taps = g_ref[0, pl.ds(base, GROUP), :]
        for r in range(GROUP):
            t = _toeplitz(taps[r : r + 1], valid)
            lhs = _lhs(shifted_ref, r, base, rows, blocks)
            acc = acc + jnp.dot(lhs, t, preferred_element_type=jnp.float32)
        return acc

    acc = lax.fori_loop(0, full, group, jnp.zeros((rows * blocks, LANES), jnp.float32))
    base = GROUP * full
    taps = g_ref[0, pl.ds(base, span - base), :]
    for r in range(span - base):
        t = _toeplitz(taps[r : r + 1], valid)
        acc = acc + jnp.dot(_lhs(shifted_ref, r, base, rows, blocks), t, preferred_element_type=jnp.float32)
    return acc


def _blur_sweep(g_ref, shifted_ref, valid, span, rows, blocks):
    tall = rows + GROUP
    full = (span - 1) // GROUP

    def pair(taps, r, base, acc):
        t = jnp.concatenate([_toeplitz(taps[r : r + 1], valid), _toeplitz(taps[r + 1 : r + 2], valid)], axis=1)
        z = jnp.dot(_lhs(shifted_ref, r, base, tall, blocks), t, preferred_element_type=jnp.float32)
        pieces = [
            z[n * tall : n * tall + rows, :LANES] + z[n * tall + 1 : n * tall + 1 + rows, LANES:]
            for n in range(blocks)
        ]
        return acc + jnp.concatenate(pieces, axis=0)

    def group(q, acc):
        base = pl.multiple_of(q * GROUP, GROUP)
        taps = g_ref[0, pl.ds(base, GROUP), :]
        for r in range(0, GROUP, 2):
            acc = pair(taps, r, base, acc)
        return acc

    acc = lax.fori_loop(0, full, group, jnp.zeros((rows * blocks, LANES), jnp.float32))
    base = GROUP * full
    taps = g_ref[0, pl.ds(base, span - base), :]
    for r in range(span - base):
        t = _toeplitz(taps[r : r + 1], valid)
        acc = acc + jnp.dot(_lhs(shifted_ref, r, base, rows, blocks), t, preferred_element_type=jnp.float32)
    return acc


def _blur_body(g_ref, x_ref, o_ref, shifted_ref, *, span, rows, blocks):
    k = pl.program_id(0)

    @pl.when(k == 0)
    def _():
        o_ref[...] = jnp.zeros_like(o_ref)

    _shift_rows(x_ref.at[0], shifted_ref)
    acc = _blur_sweep(g_ref, shifted_ref, _band(span), span, rows, blocks)
    o_ref[...] += acc


def blur(g, x, rows):
    nk, span, _ = g.shape
    src_rows, padded_width = x.shape[1], x.shape[2]
    blocks = (padded_width - LANES) // LANES
    out = pl.pallas_call(
        functools.partial(_blur_body, span=span, rows=rows, blocks=blocks),
        grid=(nk,),
        in_specs=[
            pl.BlockSpec((1, span, LANES), lambda k: (k, 0, 0)),
            pl.BlockSpec((1, src_rows, padded_width), lambda k: (k, 0, 0)),
        ],
        out_specs=pl.BlockSpec((rows * blocks, LANES), lambda k: (0, 0)),
        out_shape=jax.ShapeDtypeStruct((rows * blocks, LANES), jnp.float32),
        scratch_shapes=[pltpu.VMEM((GROUP, src_rows, padded_width), jnp.bfloat16)],
        compiler_params=pltpu.CompilerParams(dimension_semantics=("arbitrary",)),
    )(g, x)
    return jnp.concatenate([out[n * rows : (n + 1) * rows] for n in range(blocks)], axis=1)


def _back_body(g_ref, e_ref, w_ref, o_ref, shifted_ref, acc_ref, *, span, rows, blocks):
    nk = g_ref.shape[0]
    _shift_rows(e_ref, shifted_ref)
    acc_ref[...] = jnp.zeros_like(acc_ref)
    valid = _band(span)

    def step(taps, r, base):
        t = jnp.concatenate([_toeplitz(taps[k, r : r + 1], valid) for k in range(nk)], axis=1)
        lhs = _lhs(shifted_ref, r, base, rows, blocks)
        acc_ref[...] += jnp.dot(lhs, t, preferred_element_type=jnp.float32)

    full = (span - 1) // GROUP

    def group(q, carry):
        base = pl.multiple_of(q * GROUP, GROUP)
        taps = g_ref[:, pl.ds(base, GROUP), :]
        for r in range(GROUP):
            step(taps, r, base)
        return carry

    lax.fori_loop(0, full, group, 0)
    base = GROUP * full
    taps = g_ref[:, pl.ds(base, span - base), :]
    for r in range(span - base):
        step(taps, r, base)
    total = jnp.zeros(o_ref.shape, jnp.float32)
    for k in range(nk):
        back = jnp.concatenate(
            [acc_ref[n * rows : (n + 1) * rows, k * LANES : (k + 1) * LANES] for n in range(blocks)], axis=1
        )
        total = total + w_ref[k].astype(jnp.float32) * back
    o_ref[...] = total


def back_weighted(g, e, w):
    nk, span, _ = g.shape
    rows, width = w.shape[1], w.shape[2]
    blocks = width // LANES
    return pl.pallas_call(
        functools.partial(_back_body, span=span, rows=rows, blocks=blocks),
        out_shape=jax.ShapeDtypeStruct((rows, width), jnp.float32),
        scratch_shapes=[
            pltpu.VMEM((GROUP,) + e.shape, jnp.bfloat16),
            pltpu.VMEM((rows * blocks, nk * LANES), jnp.float32),
        ],
    )(g, e, w)


def per_device(
    estimate, residual, direction, kernels, weight_maps, filters_in, biases, filters_out
):
    rows, width = direction.shape
    half = (kernels.shape[1] - 1) // 2
    maps_wide = weight_maps.astype(jnp.float32)
    shaped = (maps_wide * direction[None]).astype(jnp.bfloat16)
    edges = jnp.stack([estimate, direction])
    padded, edge_before, edge_after = band_halo(shaped, edges, half, 2)
    framed_both = jnp.concatenate([edge_before, edges, edge_after], axis=1)
    framed_estimate, framed_direction = framed_both[0], framed_both[1]
    framed = jnp.pad(padded, ((0, 0), (0, 0), (half, LANES - half)))
    both_taps = tap_rows(jnp.concatenate([kernels, kernels[:, ::-1, ::-1]]))
    nk = kernels.shape[0]
    partial_value = blur(both_taps[:nk], framed, rows)
    image = pair_sum(partial_value, "comp").astype(jnp.bfloat16)
    edged = with_halo(image, (("band", 0),), half)
    edged = jnp.pad(edged, ((0, 0), (half, LANES - half)))
    local_sum = back_weighted(both_taps[nk:], edged, weight_maps)
    normal = pair_sum(local_sum, "comp")
    curved = normal + damping * direction
    old, product, cross, square = lax.psum(
        (
            jnp.sum(residual * residual),
            jnp.sum(direction * curved),
            jnp.sum(residual * curved),
            jnp.sum(curved * curved),
        ),
        "band",
    )
    alpha = old / product
    residual_next = residual - alpha * curved
    new = old - 2.0 * alpha * cross + alpha * alpha * square
    estimate_next = estimate + alpha * direction
    direction_next = residual_next + new / old * direction
    framed_next = framed_estimate + alpha * framed_direction
    framed_next = lax.dynamic_update_slice_in_dim(framed_next, estimate_next, 2, 0)
    denoised = denoise(framed_next, filters_in, biases, filters_out)
    return (estimate_next, residual_next, direction_next, denoised)


def solution(mesh):
    return jax.shard_map(
        per_device,
        mesh=mesh,
        in_specs=(
            P("band", None),
            P("band", None),
            P("band", None),
            P("comp", None, None),
            P("comp", "band", None),
            P(),
            P(),
            P(),
        ),
        out_specs=(P("band", None), P("band", None), P("band", None), P("band", "comp")),
        check_vma=False,
    )
```
